256 devices in a mesh: seq: 64 (over z, x, core), head: 4 (over y).
Axes of the slice: x: 4, y: 4, z: 8, core: 2. Of those that a mesh axis runs over, the one named last changes fastest.
Arguments:
- queries: bfloat16 [32768, 1536], P('seq', 'head'), may hold values from -6 to 6
- keys: bfloat16 [32768, 1536], P('seq', 'head'), may hold values from -6 to 6
- values: bfloat16 [32768, 1536], P('seq', 'head'), may hold values from -6 to 6
- out_weight: bfloat16 [1536, 1536], P('head'), may hold values from -0.625 to 0.625
- cotangent: bfloat16 [32768, 1536], P('seq', 'head'), may hold values from -6 to 6
- routes: int32 [64, 2], replicated, may hold values from 0 to 63, as said below
- shot_ids: int32 [32768], P('seq'), may hold values from 0 to 31, never falling along the last dimension, each value on 1 to 2048 neighbouring positions
Outputs:
- attn_out: bfloat16 [32768, 1536], P('seq', 'head')
- grad_queries: bfloat16 [32768, 1536], P('seq', 'head')
- grad_keys: bfloat16 [32768, 1536], P('seq', 'head')
- grad_values: bfloat16 [32768, 1536], P('seq', 'head')
The draws below stay inside these ranges and needn't reach their ends.
Inputs may be any that keep to these rules, and one draw needn't show every extreme that they name: routes[c, j] names a block of another device whose index of seq differs from that of block c by at most 2; the 2 routes of the blocks of one device name blocks of distinct devices.
All inputs are finite; a program needn't handle non-finite values.
Results may differ from the reference program's by a relative error of at most 0.025.
Values may be sent and summed in bfloat16 or wider, within the bound.
No kernel may reach another device: no remote copies, remote signals or barrier semaphores. Data moves between devices by JAX's collectives and lax.ppermute only.
A program may use at most 64 MiB of HBM per device.

```python
import math
import jax
import jax.numpy as jnp
import numpy as np
from jax import lax

HEAD_COUNT = 12
HEAD_DIM = 128
MODEL_WIDTH = 1536
BLOCK_LEN = 512
BLOCKS_DEV = 1
ROUTE_REACH = 2
BLOCK_COUNT = 64
TOKENS = 32768
SHOT_COUNT = 32
N_SEQ = 64


def draw_queries(key, part):
    base_draw = jnp.clip(1.3 * jax.random.normal(jax.random.fold_in(key, 1), (TOKENS, MODEL_WIDTH), jnp.float32), -6.0, 6.0)
    return base_draw.astype(jnp.bfloat16)


def draw_keys(key, part):
    base_draw = jnp.clip(1.3 * jax.random.normal(jax.random.fold_in(key, 2), (TOKENS, MODEL_WIDTH), jnp.float32), -6.0, 6.0)
    return base_draw.astype(jnp.bfloat16)


def draw_routes(key, part):
    span_width = 2 * ROUTE_REACH
    device = jnp.arange(N_SEQ, dtype=jnp.int32)[:, None]
    offset_table = jnp.concatenate([jnp.arange(-ROUTE_REACH, 0, dtype=jnp.int32), jnp.arange(1, ROUTE_REACH + 1, dtype=jnp.int32)])
    owner_dev = device + offset_table[None, :]
    in_range = (owner_dev >= 0) & (owner_dev < N_SEQ)
    column_ids = jnp.arange(span_width, dtype=jnp.int32)[None, :]
    raw_bits = jax.random.randint(jax.random.fold_in(key, 21), (N_SEQ, span_width), 0, 1 << 20)
    scores = raw_bits * span_width + column_ids
    forced_pair = (device == N_SEQ - 2) & (offset_table[None, :] == 1) | (device == 1) & (offset_table[None, :] == -1)
    scores = jnp.where(forced_pair, scores + (1 << 26), scores)
    scores = jnp.where(in_range, scores, -1 - column_ids)
    unused, chosen = lax.top_k(scores, 2 * BLOCKS_DEV)
    picked_owner = jnp.take_along_axis(owner_dev, chosen, axis=1)
    local_block = jax.random.randint(jax.random.fold_in(key, 22), (N_SEQ, 2 * BLOCKS_DEV), 0, BLOCKS_DEV)
    first_slot = jnp.arange(2 * BLOCKS_DEV, dtype=jnp.int32)[None, :] == 0
    local_block = jnp.where(first_slot & (device == N_SEQ - 2), BLOCKS_DEV - 1, local_block)
    local_block = jnp.where(first_slot & (device == 1), 0, local_block)
    return (picked_owner * BLOCKS_DEV + local_block).reshape(BLOCK_COUNT, 2).astype(jnp.int32)


def levels(own_key, extent, cuts, least, top_value):
    level, own = 1.0, jax.random.fold_in(own_key, 6)
    for dim, shards_of in cuts:
        heights = jnp.exp(jax.random.uniform(jax.random.fold_in(own, dim), (shards_of,), jnp.float32, least / len(cuts), top_value / len(cuts)))
        level = level * jnp.repeat(heights, extent[dim] // shards_of).reshape([-1 if axis == dim else 1 for axis in range(len(extent))])
    return level


def length_profile(number_of, total, bound, skew):
    weights = [(1 << 20) // math.isqrt(standing ** skew) + 1 for standing in range(2, number_of + 1)]
    rest, counts = total - bound - (number_of - 1), [1] * (number_of - 1)
    while rest > 0:
        movable = [i for i in range(number_of - 1) if counts[i] < bound]
        mass, budget = sum([weights[i] for i in movable]), rest
        for i in movable:
            addition = min(bound - counts[i], max(1, budget * weights[i] // mass), rest)
            counts[i] = counts[i] + addition
            rest = rest - addition
    return np.array([bound] + counts)


def uneven(rng, amount, total, reach, lean):
    if amount == 2:
        one = jax.random.randint(rng, (), max(1, total - reach), min(reach, total - 1) + 1)
        return jnp.stack([one, total - one])
    lengths = jnp.asarray(length_profile(amount, total, reach, lean), jnp.int32)
    pairs = (amount - 1) // 2
    giver, taker = lengths[1:1 + 2 * pairs:2], lengths[2:2 + 2 * pairs:2]
    slack = jnp.minimum(giver - 1, reach - taker)
    moved = jax.random.randint(jax.random.fold_in(rng, 1), (pairs,), 0, 1 << 20) % (slack + 1)
    lengths = lengths.at[1:1 + 2 * pairs:2].set(giver - moved).at[2:2 + 2 * pairs:2].set(taker + moved)
    return lengths[jax.random.permutation(jax.random.fold_in(rng, 2), amount)]


def bell_draw(rng, dims, spread, most, pieces=(), kind=jnp.bfloat16):
    array = jax.random.normal(rng, dims, jnp.float32) * spread
    if len(pieces) > 0:
        array = levels(rng, dims, pieces, -0.22, 0.18) * array
    return jnp.clip(array, min=-most, max=most).astype(kind)


def setup_inputs(seed: int = 0) -> dict:
    splits = jax.random.split(jax.random.key(seed), 8)
    queries = draw_queries(jax.random.fold_in(splits[7], 71), 0)
    keys = draw_keys(jax.random.fold_in(splits[7], 71), 0)
    values = bell_draw(splits[2], (TOKENS, MODEL_WIDTH), 1.0, 6.0, ((0, 64), (1, 4)))
    out_weight = bell_draw(splits[3], (MODEL_WIDTH, MODEL_WIDTH), (MODEL_WIDTH // 16) ** -0.5, 0.625, ((0, 4),))
    cotangent = bell_draw(splits[4], (TOKENS, MODEL_WIDTH), 1.0, 6.0, ((0, 64), (1, 4)))
    routes = draw_routes(jax.random.fold_in(splits[7], 71), 0)
    shot_ids = jnp.searchsorted(jnp.cumsum(uneven(splits[6], SHOT_COUNT, TOKENS, 4 * BLOCK_LEN, 2)), jnp.arange(TOKENS), side="right").astype(jnp.int32)
    return {"queries": queries, "keys": keys, "values": values, "out_weight": out_weight, "cotangent": cotangent, "routes": routes, "shot_ids": shot_ids}


def rounded(term):
    return lax.optimization_barrier(term.astype(jnp.bfloat16)).astype(jnp.float32)


def reference(queries, keys, values, out_weight, cotangent, routes, shot_ids):
    score_scale = HEAD_DIM ** -0.5
    highest = lax.Precision.HIGHEST
    weight_full = out_weight.astype(jnp.float32)
    grad_attn = jnp.dot(cotangent.astype(jnp.float32), weight_full.T, precision=highest).astype(jnp.bfloat16)
    grad_attn = lax.optimization_barrier(grad_attn)
    shape_four = (BLOCK_COUNT, BLOCK_LEN, HEAD_COUNT, HEAD_DIM)
    query_blocks = queries.reshape(shape_four)
    key_blocks = keys.reshape(shape_four)
    value_blocks = values.reshape(shape_four)
    grad_blocks = grad_attn.reshape(shape_four)
    shot_blocks = shot_ids.reshape(BLOCK_COUNT, BLOCK_LEN)
    routed_tail = jnp.ones((BLOCK_LEN, 2 * BLOCK_LEN), jnp.bool_)

    def visit(carry, block_index):
        key_sums, value_sums = carry
        first_route = routes[block_index, 0].astype(jnp.int32)
        second_route = routes[block_index, 1].astype(jnp.int32)
        query_rows = query_blocks[block_index].astype(jnp.float32)
        grad_rows = grad_blocks[block_index].astype(jnp.float32)
        key_rows = jnp.concatenate([key_blocks[block_index], key_blocks[first_route], key_blocks[second_route]], axis=0).astype(jnp.float32)
        value_rows = jnp.concatenate([value_blocks[block_index], value_blocks[first_route], value_blocks[second_route]], axis=0).astype(jnp.float32)
        shots_here = shot_blocks[block_index]
        visible = jnp.concatenate([shots_here[:, None] == shots_here[None, :], routed_tail], axis=1)
        scores = jnp.einsum("qhd,khd->hqk", query_rows, key_rows, precision=highest) * score_scale
        masked = jnp.where(visible[None], scores, -1e30)
        row_top = jnp.max(masked, axis=2, keepdims=True)
        weights = jnp.exp(masked - row_top)
        probs_full = weights / jnp.sum(weights, axis=2, keepdims=True)
        probs_wide = rounded(probs_full)
        attn_wide = rounded(jnp.einsum("hqk,khd->qhd", probs_wide, value_rows, precision=highest))
        row_dot = jnp.einsum("qhd,qhd->hq", attn_wide, grad_rows, precision=highest)
        dprobs = jnp.einsum("qhd,khd->hqk", grad_rows, value_rows, precision=highest)
        dscores_wide = rounded(probs_full * (dprobs - row_dot[:, :, None]) * score_scale)
        grad_query = jnp.einsum("hqk,khd->qhd", dscores_wide, key_rows, precision=highest).astype(jnp.bfloat16)
        key_terms = jnp.einsum("hqk,qhd->khd", dscores_wide, query_rows, precision=highest).reshape(3, BLOCK_LEN, HEAD_COUNT, HEAD_DIM)
        value_terms = jnp.einsum("hqk,qhd->khd", probs_wide, grad_rows, precision=highest).reshape(3, BLOCK_LEN, HEAD_COUNT, HEAD_DIM)
        key_sums = key_sums.at[block_index].add(key_terms[0])
        key_sums = key_sums.at[first_route].add(rounded(key_terms[1]))
        key_sums = key_sums.at[second_route].add(rounded(key_terms[2]))
        value_sums = value_sums.at[block_index].add(value_terms[0])
        value_sums = value_sums.at[first_route].add(rounded(value_terms[1]))
        value_sums = value_sums.at[second_route].add(rounded(value_terms[2]))
        return (key_sums, value_sums), (attn_wide.astype(jnp.bfloat16), grad_query)

    start_sums = (jnp.zeros(shape_four, jnp.float32), jnp.zeros(shape_four, jnp.float32))
    (key_sums, value_sums), (attn_all, query_all) = lax.scan(visit, start_sums, jnp.arange(BLOCK_COUNT, dtype=jnp.int32))
    attn_flat = attn_all.reshape(TOKENS, MODEL_WIDTH).astype(jnp.float32)
    attn_out = jnp.dot(attn_flat, weight_full, precision=highest).astype(jnp.bfloat16)
    grad_queries = query_all.reshape(TOKENS, MODEL_WIDTH)
    grad_keys = key_sums.astype(jnp.bfloat16).reshape(TOKENS, MODEL_WIDTH)
    grad_values = value_sums.astype(jnp.bfloat16).reshape(TOKENS, MODEL_WIDTH)
    return (attn_out, grad_queries, grad_keys, grad_values)
```

```python
import functools

import jax
import jax.numpy as jnp
from jax import lax
from jax.experimental import pallas as pl
from jax.experimental.pallas import tpu as pltpu
from jax.sharding import PartitionSpec as P

HEAD_DIM = 128
BLOCK_LEN = 512
NEG_BIG = -1e30
INTERPRET = None


def shifted(block, axis, distance):
    devices = range(lax.axis_size(axis))
    route = [(i - distance, i) for i in devices if i - distance in devices]
    return lax.ppermute(block, axis, route)


def partner_swap(block, axis):
    size = lax.axis_size(axis)
    return lax.ppermute(block, axis, [(i, i ^ 1) for i in range(size)])


def pack_heads(keys, values):
    rows, columns = keys.shape
    heads = columns // HEAD_DIM
    k4 = keys.reshape(rows, heads, 1, HEAD_DIM)
    v4 = values.reshape(rows, heads, 1, HEAD_DIM)
    return jnp.concatenate([k4, v4], axis=2).reshape(rows, 2 * columns)


def unpack_heads(packed):
    rows, wide = packed.shape
    heads = wide // (2 * HEAD_DIM)
    p4 = packed.reshape(rows, heads, 2, HEAD_DIM)
    return (p4[:, :, 0, :].reshape(rows, heads * HEAD_DIM), p4[:, :, 1, :].reshape(rows, heads * HEAD_DIM))


def attn_kernel(sel_ref, q_ref, kv0_ref, c0_ref, c1_ref, c2_ref, c3_ref, g_ref, srow_ref, scol_ref,
                attn_ref, dq_ref, dkv0_ref, dkv1_ref, dkv2_ref):
    scale = HEAD_DIM ** (-0.5)
    d = HEAD_DIM
    cands = (c0_ref, c1_ref, c2_ref, c3_ref)

    def pick(slot):
        idx = sel_ref[slot]
        out = cands[0][...]
        for c in range(1, 4):
            out = jnp.where(idx == c, cands[c][...], out)
        return out

    kv = [kv0_ref[...], pick(0), pick(1)]
    ks = [x[:, :d] for x in kv]
    vs = [x[:, d:] for x in kv]
    q = q_ref[...]
    g = g_ref[...]
    nt = (((1,), (1,)), ((), ()))
    tn = (((0,), (0,)), ((), ()))
    scores = [lax.dot_general(q, k, nt, preferred_element_type=jnp.float32) * scale for k in ks]
    visible = srow_ref[...] == scol_ref[...]
    scores[0] = jnp.where(visible, scores[0], NEG_BIG)
    top = jnp.max(scores[0], axis=1, keepdims=True)
    for s in scores[1:]:
        top = jnp.maximum(top, jnp.max(s, axis=1, keepdims=True))
    weights = [jnp.exp(s - top) for s in scores]
    weights[0] = jnp.where(visible, weights[0], 0.0)
    total = weights[0].sum(axis=1, keepdims=True)
    for w in weights[1:]:
        total = total + w.sum(axis=1, keepdims=True)
    inv = 1.0 / total
    probs = [w * inv for w in weights]
    low = [p.astype(jnp.bfloat16) for p in probs]
    acc = jnp.dot(low[0], vs[0], preferred_element_type=jnp.float32)
    for j in (1, 2):
        acc = acc + jnp.dot(low[j], vs[j], preferred_element_type=jnp.float32)
    attn = acc.astype(jnp.bfloat16)
    attn_ref[...] = attn
    gf = g.astype(jnp.float32)
    delta = jnp.sum(attn.astype(jnp.float32) * gf, axis=1, keepdims=True)
    dq = None
    outs = (dkv0_ref, dkv1_ref, dkv2_ref)
    for j in range(3):
        dp = lax.dot_general(g, vs[j], nt, preferred_element_type=jnp.float32)
        ds = (probs[j] * (dp - delta) * scale).astype(jnp.bfloat16)
        part = jnp.dot(ds, ks[j], preferred_element_type=jnp.float32)
        dq = part if dq is None else dq + part
        dk = lax.dot_general(ds, q, tn, preferred_element_type=jnp.float32)
        dv = lax.dot_general(low[j], g, tn, preferred_element_type=jnp.float32)
        outs[j][:, :d] = dk.astype(outs[j].dtype)
        outs[j][:, d:] = dv.astype(outs[j].dtype)
    dq_ref[...] = dq.astype(jnp.bfloat16)


def attention(sel, queries, kv_self, cands, grad_attn, shot_ids):
    rows, columns = queries.shape
    heads = columns // HEAD_DIM
    d = HEAD_DIM
    col = lambda h, s: (0, h)
    spec_q = pl.BlockSpec((rows, d), col)
    spec_kv = pl.BlockSpec((rows, 2 * d), col)
    grid_spec = pltpu.PrefetchScalarGridSpec(
        num_scalar_prefetch=1,
        grid=(heads,),
        in_specs=[spec_q, spec_kv, spec_kv, spec_kv, spec_kv, spec_kv, spec_q,
                  pl.BlockSpec((rows, 1), lambda h, s: (0, 0)),
                  pl.BlockSpec((1, rows), lambda h, s: (0, 0))],
        out_specs=[spec_q, spec_q, spec_kv, spec_kv, spec_kv],
    )
    out_shape = [
        jax.ShapeDtypeStruct((rows, columns), jnp.bfloat16),
        jax.ShapeDtypeStruct((rows, columns), jnp.bfloat16),
        jax.ShapeDtypeStruct((rows, 2 * columns), jnp.float32),
        jax.ShapeDtypeStruct((rows, 2 * columns), jnp.bfloat16),
        jax.ShapeDtypeStruct((rows, 2 * columns), jnp.bfloat16),
    ]
    kwargs = {}
    if INTERPRET is not None:
        kwargs["interpret"] = INTERPRET
    return pl.pallas_call(
        attn_kernel,
        grid_spec=grid_spec,
        out_shape=out_shape,
        compiler_params=pltpu.CompilerParams(vmem_limit_bytes=48 * 1024 * 1024),
        **kwargs,
    )(sel, queries, kv_self, *cands, grad_attn, shot_ids.reshape(rows, 1), shot_ids.reshape(1, rows))


def on_device(queries, keys, values, out_weight, cotangent, routes, shot_ids):
    seq_index = lax.axis_index("seq")
    tok_rows, columns = queries.shape
    parity = seq_index % 2
    cot_full = lax.all_gather(cotangent, "head", axis=1, tiled=True)
    grad_attn = lax.dot_general(
        cot_full, out_weight, (((1,), (1,)), ((), ())), preferred_element_type=jnp.float32
    ).astype(jnp.bfloat16)
    own_kv = pack_heads(keys, values)
    from_left2 = shifted(own_kv, "seq", 2)
    from_right2 = shifted(own_kv, "seq", -2)
    partner_own = partner_swap(own_kv, "seq")
    relay_out = jnp.where(parity == 0, from_right2, from_left2)
    partner_relay = partner_swap(relay_out, "seq")
    partner_off = 1 - 2 * parity
    offs = routes[seq_index] - seq_index
    sel = jnp.where(offs == -2, 0, jnp.where(offs == 2, 3, jnp.where(offs == partner_off, 1, 2)))
    sel = sel.astype(jnp.int32)
    cands = (from_left2, partner_own, partner_relay, from_right2)
    attn, grad_q, self_term, term1, term2 = attention(sel, queries, own_kv, cands, grad_attn, shot_ids)
    partial_out = jnp.dot(attn, out_weight, preferred_element_type=jnp.float32)
    attn_out = lax.psum_scatter(partial_out.astype(jnp.bfloat16), "head", scatter_dimension=1, tiled=True)
    zero = jnp.zeros_like(term1)

    def term_for(offset):
        return jnp.where(offs[0] == offset, term1, jnp.where(offs[1] == offset, term2, zero))

    t_plus1 = term_for(1)
    t_minus1 = term_for(-1)
    to_partner_own = jnp.where(parity == 0, t_plus1, t_minus1)
    to_partner_relay = jnp.where(parity == 0, t_minus1, t_plus1)
    back_own = partner_swap(to_partner_own, "seq")
    back_relay = partner_swap(to_partner_relay, "seq").astype(jnp.float32)
    up_plus = term_for(2).astype(jnp.float32) + jnp.where(parity == 0, back_relay, 0.0)
    up_minus = term_for(-2).astype(jnp.float32) + jnp.where(parity == 1, back_relay, 0.0)
    got_from_left = shifted(up_plus.astype(jnp.bfloat16), "seq", 2)
    got_from_right = shifted(up_minus.astype(jnp.bfloat16), "seq", -2)
    total = (
        self_term
        + back_own.astype(jnp.float32)
        + got_from_left.astype(jnp.float32)
        + got_from_right.astype(jnp.float32)
    )
    grad_keys, grad_values = unpack_heads(total.astype(jnp.bfloat16))
    return (attn_out, grad_q, grad_keys, grad_values)


def solution(mesh):
    in_specs = (
        P("seq", "head"),
        P("seq", "head"),
        P("seq", "head"),
        P("head", None),
        P("seq", "head"),
        P(),
        P("seq"),
    )
    out_specs = (P("seq", "head"), P("seq", "head"), P("seq", "head"), P("seq", "head"))
    return jax.shard_map(
        on_device, mesh=mesh, in_specs=in_specs, out_specs=out_specs, check_vma=False
    )
```

```python
import functools

import jax
import jax.numpy as jnp
from jax import lax
from jax.experimental import pallas as pl
from jax.experimental.pallas import tpu as pltpu
from jax.sharding import PartitionSpec as P

HEAD_DIM = 128
BLOCK_LEN = 512
NEG_BIG = -1e30
INTERPRET = None


def shifted(block, axis, distance):
    devices = range(lax.axis_size(axis))
    route = [(i - distance, i) for i in devices if i - distance in devices]
    return lax.ppermute(block, axis, route)


def ring_shift(block, axis, distance):
    size = lax.axis_size(axis)
    return lax.ppermute(block, axis, [(i, (i + distance) % size) for i in range(size)])


def head_slice(array, group, width):
    return lax.dynamic_slice_in_dim(array, group * width, width, 1)


def fold_cotangent(cotangent, out_weight):
    groups = lax.axis_size("head")
    me = lax.axis_index("head")
    rows, width = cotangent.shape
    half = rows // 2
    from_prev = ring_shift(cotangent, "head", 1)
    from_next = ring_shift(cotangent, "head", -1)
    far_a = ring_shift(from_prev[:half], "head", 1)
    far_b = ring_shift(from_next[half:], "head", -1)
    far = jnp.concatenate([far_a, far_b], axis=0)
    nt = (((1,), (1,)), ((), ()))
    acc = None
    for piece, group in ((cotangent, me), (from_prev, me - 1), (from_next, me + 1), (far, me + 2)):
        w_cols = head_slice(out_weight, group % groups, width)
        part = lax.dot_general(piece, w_cols, nt, preferred_element_type=jnp.float32)
        acc = part if acc is None else acc + part
    return acc.astype(jnp.bfloat16)


def project_out(attn, out_weight):
    groups = lax.axis_size("head")
    me = lax.axis_index("head")
    rows, width = attn.shape
    half = rows // 2

    def part(group):
        w_cols = head_slice(out_weight, group % groups, width)
        return jnp.dot(attn, w_cols, preferred_element_type=jnp.float32)

    far = part(me + 2).astype(jnp.bfloat16)
    got_a = ring_shift(far[:half], "head", 1)
    got_b = ring_shift(far[half:], "head", -1)
    zeros = jnp.zeros((half, width), jnp.float32)
    up = part(me + 1) + jnp.concatenate([got_a.astype(jnp.float32), zeros], axis=0)
    down = part(me - 1) + jnp.concatenate([zeros, got_b.astype(jnp.float32)], axis=0)
    from_prev = ring_shift(up.astype(jnp.bfloat16), "head", 1)
    from_next = ring_shift(down.astype(jnp.bfloat16), "head", -1)
    total = part(me) + from_prev.astype(jnp.float32) + from_next.astype(jnp.float32)
    return total.astype(jnp.bfloat16)


def partner_swap(block, axis):
    size = lax.axis_size(axis)
    return lax.ppermute(block, axis, [(i, i ^ 1) for i in range(size)])


def pack_heads(keys, values):
    rows, columns = keys.shape
    heads = columns // HEAD_DIM
    k4 = keys.reshape(rows, heads, 1, HEAD_DIM)
    v4 = values.reshape(rows, heads, 1, HEAD_DIM)
    return jnp.concatenate([k4, v4], axis=2).reshape(rows, 2 * columns)


def unpack_heads(packed):
    rows, wide = packed.shape
    heads = wide // (2 * HEAD_DIM)
    p4 = packed.reshape(rows, heads, 2, HEAD_DIM)
    return (p4[:, :, 0, :].reshape(rows, heads * HEAD_DIM), p4[:, :, 1, :].reshape(rows, heads * HEAD_DIM))


def attn_kernel(sel_ref, q_ref, kv0_ref, c0_ref, c1_ref, c2_ref, c3_ref, g_ref, srow_ref, scol_ref,
                attn_ref, dq_ref, dkv0_ref, dkv1_ref, dkv2_ref):
    scale = HEAD_DIM ** (-0.5)
    d = HEAD_DIM
    cands = (c0_ref, c1_ref, c2_ref, c3_ref)

    def pick(slot):
        idx = sel_ref[slot]
        out = cands[0][...]
        for c in range(1, 4):
            out = jnp.where(idx == c, cands[c][...], out)
        return out

    kv = [kv0_ref[...], pick(0), pick(1)]
    ks = [x[:, :d] for x in kv]
    vs = [x[:, d:] for x in kv]
    q = q_ref[...]
    g = g_ref[...]
    nt = (((1,), (1,)), ((), ()))
    tn = (((0,), (0,)), ((), ()))
    scores = [lax.dot_general(q, k, nt, preferred_element_type=jnp.float32) * scale for k in ks]
    visible = srow_ref[...] == scol_ref[...]
    scores[0] = jnp.where(visible, scores[0], NEG_BIG)
    top = jnp.max(scores[0], axis=1, keepdims=True)
    for s in scores[1:]:
        top = jnp.maximum(top, jnp.max(s, axis=1, keepdims=True))
    weights = [jnp.exp(s - top) for s in scores]
    weights[0] = jnp.where(visible, weights[0], 0.0)
    total = weights[0].sum(axis=1, keepdims=True)
    for w in weights[1:]:
        total = total + w.sum(axis=1, keepdims=True)
    inv = 1.0 / total
    probs = [w * inv for w in weights]
    low = [p.astype(jnp.bfloat16) for p in probs]
    acc = jnp.dot(low[0], vs[0], preferred_element_type=jnp.float32)
    for j in (1, 2):
        acc = acc + jnp.dot(low[j], vs[j], preferred_element_type=jnp.float32)
    attn = acc.astype(jnp.bfloat16)
    attn_ref[...] = attn
    gf = g.astype(jnp.float32)
    delta = jnp.sum(attn.astype(jnp.float32) * gf, axis=1, keepdims=True)
    dq = None
    outs = (dkv0_ref, dkv1_ref, dkv2_ref)
    for j in range(3):
        dp = lax.dot_general(g, vs[j], nt, preferred_element_type=jnp.float32)
        ds = (probs[j] * (dp - delta) * scale).astype(jnp.bfloat16)
        part = jnp.dot(ds, ks[j], preferred_element_type=jnp.float32)
        dq = part if dq is None else dq + part
        dk = lax.dot_general(ds, q, tn, preferred_element_type=jnp.float32)
        dv = lax.dot_general(low[j], g, tn, preferred_element_type=jnp.float32)
        outs[j][:, :d] = dk.astype(outs[j].dtype)
        outs[j][:, d:] = dv.astype(outs[j].dtype)
    dq_ref[...] = dq.astype(jnp.bfloat16)


def attention(sel, queries, kv_self, cands, grad_attn, shot_ids):
    rows, columns = queries.shape
    heads = columns // HEAD_DIM
    d = HEAD_DIM
    col = lambda h, s: (0, h)
    spec_q = pl.BlockSpec((rows, d), col)
    spec_kv = pl.BlockSpec((rows, 2 * d), col)
    grid_spec = pltpu.PrefetchScalarGridSpec(
        num_scalar_prefetch=1,
        grid=(heads,),
        in_specs=[spec_q, spec_kv, spec_kv, spec_kv, spec_kv, spec_kv, spec_q,
                  pl.BlockSpec((rows, 1), lambda h, s: (0, 0)),
                  pl.BlockSpec((1, rows), lambda h, s: (0, 0))],
        out_specs=[spec_q, spec_q, spec_kv, spec_kv, spec_kv],
    )
    out_shape = [
        jax.ShapeDtypeStruct((rows, columns), jnp.bfloat16),
        jax.ShapeDtypeStruct((rows, columns), jnp.bfloat16),
        jax.ShapeDtypeStruct((rows, 2 * columns), jnp.float32),
        jax.ShapeDtypeStruct((rows, 2 * columns), jnp.bfloat16),
        jax.ShapeDtypeStruct((rows, 2 * columns), jnp.bfloat16),
    ]
    kwargs = {}
    if INTERPRET is not None:
        kwargs["interpret"] = INTERPRET
    return pl.pallas_call(
        attn_kernel,
        grid_spec=grid_spec,
        out_shape=out_shape,
        compiler_params=pltpu.CompilerParams(vmem_limit_bytes=48 * 1024 * 1024),
        **kwargs,
    )(sel, queries, kv_self, *cands, grad_attn, shot_ids.reshape(rows, 1), shot_ids.reshape(1, rows))


def on_device(queries, keys, values, out_weight, cotangent, routes, shot_ids):
    seq_index = lax.axis_index("seq")
    tok_rows, columns = queries.shape
    parity = seq_index % 2
    grad_attn = fold_cotangent(cotangent, out_weight)
    own_kv = pack_heads(keys, values)
    from_left2 = shifted(own_kv, "seq", 2)
    from_right2 = shifted(own_kv, "seq", -2)
    partner_own = partner_swap(own_kv, "seq")
    relay_out = jnp.where(parity == 0, from_right2, from_left2)
    partner_relay = partner_swap(relay_out, "seq")
    partner_off = 1 - 2 * parity
    offs = routes[seq_index] - seq_index
    sel = jnp.where(offs == -2, 0, jnp.where(offs == 2, 3, jnp.where(offs == partner_off, 1, 2)))
    sel = sel.astype(jnp.int32)
    cands = (from_left2, partner_own, partner_relay, from_right2)
    attn, grad_q, self_term, term1, term2 = attention(sel, queries, own_kv, cands, grad_attn, shot_ids)
    attn_out = project_out(attn, out_weight)
    zero = jnp.zeros_like(term1)

    def term_for(offset):
        return jnp.where(offs[0] == offset, term1, jnp.where(offs[1] == offset, term2, zero))

    t_plus1 = term_for(1)
    t_minus1 = term_for(-1)
    to_partner_own = jnp.where(parity == 0, t_plus1, t_minus1)
    to_partner_relay = jnp.where(parity == 0, t_minus1, t_plus1)
    back_own = partner_swap(to_partner_own, "seq")
    back_relay = partner_swap(to_partner_relay, "seq").astype(jnp.float32)
    up_plus = term_for(2).astype(jnp.float32) + jnp.where(parity == 0, back_relay, 0.0)
    up_minus = term_for(-2).astype(jnp.float32) + jnp.where(parity == 1, back_relay, 0.0)
    got_from_left = shifted(up_plus.astype(jnp.bfloat16), "seq", 2)
    got_from_right = shifted(up_minus.astype(jnp.bfloat16), "seq", -2)
    total = (
        self_term
        + back_own.astype(jnp.float32)
        + got_from_left.astype(jnp.float32)
        + got_from_right.astype(jnp.float32)
    )
    grad_keys, grad_values = unpack_heads(total.astype(jnp.bfloat16))
    return (attn_out, grad_q, grad_keys, grad_values)


def solution(mesh):
    in_specs = (
        P("seq", "head"),
        P("seq", "head"),
        P("seq", "head"),
        P("head", None),
        P("seq", "head"),
        P(),
        P("seq"),
    )
    out_specs = (P("seq", "head"), P("seq", "head"), P("seq", "head"), P("seq", "head"))
    return jax.shard_map(
        on_device, mesh=mesh, in_specs=in_specs, out_specs=out_specs, check_vma=False
    )
```

```python
import jax
import jax.numpy as jnp
from jax import lax
from jax.experimental import pallas as pl
from jax.experimental.pallas import tpu as pltpu
from jax.sharding import PartitionSpec as P

HEAD_DIM = 128
BLOCK_LEN = 512
NEG_BIG = -1e30
INTERPRET = None


def shifted(block, axis, distance):
    devices = range(lax.axis_size(axis))
    route = [(i - distance, i) for i in devices if i - distance in devices]
    return lax.ppermute(block, axis, route)


def ring_shift(block, axis, distance):
    size = lax.axis_size(axis)
    return lax.ppermute(block, axis, [(i, (i + distance) % size) for i in range(size)])


def head_slice(array, group, width):
    return lax.dynamic_slice_in_dim(array, group * width, width, 1)


def fold_cotangent(cotangent, out_weight):
    groups = lax.axis_size("head")
    me = lax.axis_index("head")
    rows, width = cotangent.shape
    half = rows // 2
    from_prev = ring_shift(cotangent, "head", 1)
    from_next = ring_shift(cotangent, "head", -1)
    far_a = ring_shift(cotangent[:half], "head", 2)
    far_b = ring_shift(cotangent[half:], "head", -2)
    far = jnp.concatenate([far_a, far_b], axis=0)
    nt = (((1,), (1,)), ((), ()))
    acc = None
    for piece, group in ((cotangent, me), (from_prev, me - 1), (from_next, me + 1), (far, me + 2)):
        w_cols = head_slice(out_weight, group % groups, width)
        part = lax.dot_general(piece, w_cols, nt, preferred_element_type=jnp.float32)
        acc = part if acc is None else acc + part
    return acc.astype(jnp.bfloat16)


def project_out(attn, out_weight):
    groups = lax.axis_size("head")
    me = lax.axis_index("head")
    rows, width = attn.shape
    half = rows // 2

    def part(group):
        w_cols = head_slice(out_weight, group % groups, width)
        return jnp.dot(attn, w_cols, preferred_element_type=jnp.float32).astype(jnp.bfloat16)

    far = part(me + 2)
    got_a = ring_shift(far[:half], "head", 2)
    got_b = ring_shift(far[half:], "head", -2)
    from_prev = ring_shift(part(me + 1), "head", 1)
    from_next = ring_shift(part(me - 1), "head", -1)
    total = (
        jnp.dot(attn, head_slice(out_weight, me, width), preferred_element_type=jnp.float32)
        + from_prev.astype(jnp.float32)
        + from_next.astype(jnp.float32)
        + jnp.concatenate([got_a, got_b], axis=0).astype(jnp.float32)
    )
    return total.astype(jnp.bfloat16)


def partner_swap(block, axis):
    size = lax.axis_size(axis)
    return lax.ppermute(block, axis, [(i, i ^ 1) for i in range(size)])


def attn_kernel(sel_ref, q_ref, k0_ref, v0_ref, *refs):
    cand_k = refs[0:8:2]
    cand_v = refs[1:8:2]
    g_ref, srow_ref, scol_ref, attn_ref, dq_ref, dkv0_ref, dkv1_ref, dkv2_ref = refs[8:]
    scale = HEAD_DIM ** (-0.5)
    d = HEAD_DIM
    h = pl.program_id(0)
    heads = pl.num_programs(0)

    def pick(cands, slot):
        idx = sel_ref[slot]
        out = cands[0][...]
        for c in range(1, 4):
            out = jnp.where(idx == c, cands[c][...], out)
        return out

    ks = [k0_ref[...], pick(cand_k, 0), pick(cand_k, 1)]
    vs = [v0_ref[...], pick(cand_v, 0), pick(cand_v, 1)]
    q = q_ref[...]
    g = g_ref[...]
    nt = (((1,), (1,)), ((), ()))
    tn = (((0,), (0,)), ((), ()))
    scores = [lax.dot_general(q, k, nt, preferred_element_type=jnp.float32) * scale for k in ks]
    visible = srow_ref[...] == scol_ref[...]
    scores[0] = jnp.where(visible, scores[0], NEG_BIG)
    top = jnp.max(scores[0], axis=1, keepdims=True)
    for s in scores[1:]:
        top = jnp.maximum(top, jnp.max(s, axis=1, keepdims=True))
    weights = [jnp.exp(s - top) for s in scores]
    weights[0] = jnp.where(visible, weights[0], 0.0)
    total = weights[0].sum(axis=1, keepdims=True)
    for w in weights[1:]:
        total = total + w.sum(axis=1, keepdims=True)
    inv = 1.0 / total
    probs = [w * inv for w in weights]
    low = [p.astype(jnp.bfloat16) for p in probs]
    acc = jnp.dot(low[0], vs[0], preferred_element_type=jnp.float32)
    for j in (1, 2):
        acc = acc + jnp.dot(low[j], vs[j], preferred_element_type=jnp.float32)
    attn = acc.astype(jnp.bfloat16)
    attn_ref[...] = attn
    gf = g.astype(jnp.float32)
    delta = jnp.sum(attn.astype(jnp.float32) * gf, axis=1, keepdims=True)
    dq = None
    outs = (dkv0_ref, dkv1_ref, dkv2_ref)
    k_cols = pl.ds(pl.multiple_of(h * d, d), d)
    v_cols = pl.ds(pl.multiple_of((heads + h) * d, d), d)
    for j in range(3):
        dp = lax.dot_general(g, vs[j], nt, preferred_element_type=jnp.float32)
        ds = (probs[j] * (dp - delta) * scale).astype(jnp.bfloat16)
        part = jnp.dot(ds, ks[j], preferred_element_type=jnp.float32)
        dq = part if dq is None else dq + part
        dk = lax.dot_general(ds, q, tn, preferred_element_type=jnp.float32)
        dv = lax.dot_general(low[j], g, tn, preferred_element_type=jnp.float32)
        outs[j][:, k_cols] = dk.astype(outs[j].dtype)
        outs[j][:, v_cols] = dv.astype(outs[j].dtype)
    dq_ref[...] = dq.astype(jnp.bfloat16)


def attention(sel, queries, keys, values, cands, grad_attn, shot_ids):
    rows, columns = queries.shape
    heads = columns // HEAD_DIM
    d = HEAD_DIM
    spec_q = pl.BlockSpec((rows, d), lambda h, s: (0, h))
    spec_v = pl.BlockSpec((rows, d), lambda h, s: (0, heads + h))
    spec_wide = pl.BlockSpec((rows, 2 * columns), lambda h, s: (0, 0))
    cand_specs = []
    cand_args = []
    for c in cands:
        cand_specs += [spec_q, spec_v]
        cand_args += [c, c]
    grid_spec = pltpu.PrefetchScalarGridSpec(
        num_scalar_prefetch=1,
        grid=(heads,),
        in_specs=[spec_q, spec_q, spec_q] + cand_specs + [spec_q,
                  pl.BlockSpec((rows, 1), lambda h, s: (0, 0)),
                  pl.BlockSpec((1, rows), lambda h, s: (0, 0))],
        out_specs=[spec_q, spec_q, spec_wide, spec_wide, spec_wide],
    )
    out_shape = [
        jax.ShapeDtypeStruct((rows, columns), jnp.bfloat16),
        jax.ShapeDtypeStruct((rows, columns), jnp.bfloat16),
        jax.ShapeDtypeStruct((rows, 2 * columns), jnp.float32),
        jax.ShapeDtypeStruct((rows, 2 * columns), jnp.bfloat16),
        jax.ShapeDtypeStruct((rows, 2 * columns), jnp.bfloat16),
    ]
    kwargs = {}
    if INTERPRET is not None:
        kwargs["interpret"] = INTERPRET
    return pl.pallas_call(
        attn_kernel,
        grid_spec=grid_spec,
        out_shape=out_shape,
        compiler_params=pltpu.CompilerParams(vmem_limit_bytes=48 * 1024 * 1024),
        **kwargs,
    )(sel, queries, keys, values, *cand_args, grad_attn, shot_ids.reshape(rows, 1), shot_ids.reshape(1, rows))


def on_device(queries, keys, values, out_weight, cotangent, routes, shot_ids):
    seq_index = lax.axis_index("seq")
    tok_rows, columns = queries.shape
    parity = seq_index % 2
    grad_attn = fold_cotangent(cotangent, out_weight)
    own_kv = jnp.concatenate([keys, values], axis=1)
    from_left2 = shifted(own_kv, "seq", 2)
    from_right2 = shifted(own_kv, "seq", -2)
    partner_own = partner_swap(own_kv, "seq")
    relay_out = jnp.where(parity == 0, from_right2, from_left2)
    partner_relay = partner_swap(relay_out, "seq")
    partner_off = 1 - 2 * parity
    offs = routes[seq_index] - seq_index
    sel = jnp.where(offs == -2, 0, jnp.where(offs == 2, 3, jnp.where(offs == partner_off, 1, 2)))
    sel = sel.astype(jnp.int32)
    cands = (from_left2, partner_own, partner_relay, from_right2)
    attn, grad_q, self_term, term1, term2 = attention(sel, queries, keys, values, cands, grad_attn, shot_ids)
    attn_out = project_out(attn, out_weight)
    zero = jnp.zeros_like(term1)

    def term_for(offset):
        return jnp.where(offs[0] == offset, term1, jnp.where(offs[1] == offset, term2, zero))

    t_plus1 = term_for(1)
    t_minus1 = term_for(-1)
    to_partner_own = jnp.where(parity == 0, t_plus1, t_minus1)
    to_partner_relay = jnp.where(parity == 0, t_minus1, t_plus1)
    back_own = partner_swap(to_partner_own, "seq")
    back_relay = partner_swap(to_partner_relay, "seq").astype(jnp.float32)
    up_plus = term_for(2).astype(jnp.float32) + jnp.where(parity == 0, back_relay, 0.0)
    up_minus = term_for(-2).astype(jnp.float32) + jnp.where(parity == 1, back_relay, 0.0)
    got_from_left = shifted(up_plus.astype(jnp.bfloat16), "seq", 2)
    got_from_right = shifted(up_minus.astype(jnp.bfloat16), "seq", -2)
    total = (
        self_term
        + back_own.astype(jnp.float32)
        + got_from_left.astype(jnp.float32)
        + got_from_right.astype(jnp.float32)
    )
    rounded = total.astype(jnp.bfloat16)
    grad_keys, grad_values = rounded[:, :columns], rounded[:, columns:]
    return (attn_out, grad_q, grad_keys, grad_values)


def solution(mesh):
    in_specs = (
        P("seq", "head"),
        P("seq", "head"),
        P("seq", "head"),
        P("head", None),
        P("seq", "head"),
        P(),
        P("seq"),
    )
    out_specs = (P("seq", "head"), P("seq", "head"), P("seq", "head"), P("seq", "head"))
    return jax.shard_map(
        on_device, mesh=mesh, in_specs=in_specs, out_specs=out_specs, check_vma=False
    )
```

```python
import jax
import jax.numpy as jnp
from jax import lax
from jax.experimental import pallas as pl
from jax.experimental.pallas import tpu as pltpu
from jax.sharding import PartitionSpec as P

HEAD_DIM = 128
BLOCK_LEN = 512
NEG_BIG = -1e30
INTERPRET = None


def shifted(block, axis, distance):
    devices = range(lax.axis_size(axis))
    route = [(i - distance, i) for i in devices if i - distance in devices]
    return lax.ppermute(block, axis, route)


def ring_shift(block, axis, distance):
    size = lax.axis_size(axis)
    return lax.ppermute(block, axis, [(i, (i + distance) % size) for i in range(size)])


def head_slice(array, group, width):
    return lax.dynamic_slice_in_dim(array, group * width, width, 1)


def fold_cotangent(cotangent, out_weight):
    groups = lax.axis_size("head")
    me = lax.axis_index("head")
    rows, width = cotangent.shape
    half = rows // 2
    from_prev = ring_shift(cotangent, "head", 1)
    from_next = ring_shift(cotangent, "head", -1)
    far_a = ring_shift(cotangent[:half], "head", 2)
    far_b = ring_shift(cotangent[half:], "head", -2)
    far = jnp.concatenate([far_a, far_b], axis=0)
    nt = (((1,), (1,)), ((), ()))
    acc = None
    for piece, group in ((cotangent, me), (from_prev, me - 1), (from_next, me + 1), (far, me + 2)):
        w_cols = head_slice(out_weight, group % groups, width)
        part = lax.dot_general(piece, w_cols, nt, preferred_element_type=jnp.float32)
        acc = part if acc is None else acc + part
    return acc.astype(jnp.bfloat16)


def project_out(attn, out_weight):
    groups = lax.axis_size("head")
    me = lax.axis_index("head")
    rows, width = attn.shape
    half = rows // 2

    def part(group):
        w_cols = head_slice(out_weight, group % groups, width)
        return jnp.dot(attn, w_cols, preferred_element_type=jnp.float32).astype(jnp.bfloat16)

    far = part(me + 2)
    got_a = ring_shift(far[:half], "head", 2)
    got_b = ring_shift(far[half:], "head", -2)
    from_prev = ring_shift(part(me + 1), "head", 1)
    from_next = ring_shift(part(me - 1), "head", -1)
    total = (
        jnp.dot(attn, head_slice(out_weight, me, width), preferred_element_type=jnp.float32)
        + from_prev.astype(jnp.float32)
        + from_next.astype(jnp.float32)
        + jnp.concatenate([got_a, got_b], axis=0).astype(jnp.float32)
    )
    return total.astype(jnp.bfloat16)


def partner_swap(block, axis):
    size = lax.axis_size(axis)
    return lax.ppermute(block, axis, [(i, i ^ 1) for i in range(size)])


def even_to_odd(block, axis):
    size = lax.axis_size(axis)
    return lax.ppermute(block, axis, [(i, i + 1) for i in range(0, size - 1, 2)])


def odd_to_even(block, axis):
    size = lax.axis_size(axis)
    return lax.ppermute(block, axis, [(i, i - 1) for i in range(1, size, 2)])


def attn_kernel(sel_ref, q_ref, k0_ref, v0_ref, *refs):
    n_cand = 5
    cand_k = refs[0:2 * n_cand:2]
    cand_v = refs[1:2 * n_cand:2]
    g_ref, srow_ref, scol_ref, attn_ref, dq_ref, self_ref, pa_ref, pb_ref, far_ref = refs[2 * n_cand:]
    scale = HEAD_DIM ** (-0.5)
    d = HEAD_DIM
    h = pl.program_id(0)

    @pl.when(h == 0)
    def _():
        pa_ref[...] = jnp.zeros_like(pa_ref)
        pb_ref[...] = jnp.zeros_like(pb_ref)
        far_ref[...] = jnp.zeros_like(far_ref)

    def pick(cands, slot):
        idx = sel_ref[slot]
        out = cands[0][...]
        for c in range(1, n_cand):
            out = jnp.where(idx == c, cands[c][...], out)
        return out

    ks = [k0_ref[...], pick(cand_k, 0), pick(cand_k, 1)]
    vs = [v0_ref[...], pick(cand_v, 0), pick(cand_v, 1)]
    q = q_ref[...]
    g = g_ref[...]
    nt = (((1,), (1,)), ((), ()))
    tn = (((0,), (0,)), ((), ()))
    scores = [lax.dot_general(q, k, nt, preferred_element_type=jnp.float32) * scale for k in ks]
    visible = srow_ref[...] == scol_ref[...]
    scores[0] = jnp.where(visible, scores[0], NEG_BIG)
    top = jnp.max(scores[0], axis=1, keepdims=True)
    for s in scores[1:]:
        top = jnp.maximum(top, jnp.max(s, axis=1, keepdims=True))
    weights = [jnp.exp(s - top) for s in scores]
    weights[0] = jnp.where(visible, weights[0], 0.0)
    total = weights[0].sum(axis=1, keepdims=True)
    for w in weights[1:]:
        total = total + w.sum(axis=1, keepdims=True)
    inv = 1.0 / total
    probs = [w * inv for w in weights]
    low = [p.astype(jnp.bfloat16) for p in probs]
    acc = jnp.dot(low[0], vs[0], preferred_element_type=jnp.float32)
    for j in (1, 2):
        acc = acc + jnp.dot(low[j], vs[j], preferred_element_type=jnp.float32)
    attn = acc.astype(jnp.bfloat16)
    attn_ref[...] = attn
    gf = g.astype(jnp.float32)
    delta = jnp.sum(attn.astype(jnp.float32) * gf, axis=1, keepdims=True)
    dq = None
    cols = pl.ds(pl.multiple_of(h * d, d), d)
    for j in range(3):
        dp = lax.dot_general(g, vs[j], nt, preferred_element_type=jnp.float32)
        ds = (probs[j] * (dp - delta) * scale).astype(jnp.bfloat16)
        part = jnp.dot(ds, ks[j], preferred_element_type=jnp.float32)
        dq = part if dq is None else dq + part
        dk = lax.dot_general(ds, q, tn, preferred_element_type=jnp.float32)
        dv = lax.dot_general(low[j], g, tn, preferred_element_type=jnp.float32)
        if j == 0:
            self_ref[0] = dk
            self_ref[1] = dv
            continue
        dk = dk.astype(jnp.bfloat16)
        dv = dv.astype(jnp.bfloat16)
        off = sel_ref[2 + j]
        for value, dests in ((-2, ((far_ref, 0),)), (2, ((far_ref, 1),)),
                             (1, ((pa_ref, 0), (pb_ref, 1))), (-1, ((pa_ref, 1), (pb_ref, 0)))):
            @pl.when(off == value)
            def _():
                for ref, slot in dests:
                    ref[slot, 0, :, cols] = dk
                    ref[slot, 1, :, cols] = dv
    dq_ref[...] = dq.astype(jnp.bfloat16)


def attention(sel, queries, keys, values, cands, grad_attn, shot_ids):
    rows, columns = queries.shape
    heads = columns // HEAD_DIM
    d = HEAD_DIM
    spec_q = pl.BlockSpec((rows, d), lambda h, s: (0, h))
    spec_ck = pl.BlockSpec((None, rows, d), lambda h, s: (0, 0, h))
    spec_cv = pl.BlockSpec((None, rows, d), lambda h, s: (1, 0, h))
    spec_self = pl.BlockSpec((2, rows, d), lambda h, s: (0, 0, h))
    spec_pair = pl.BlockSpec((2, 2, rows, columns), lambda h, s: (0, 0, 0, 0))
    cand_specs = []
    cand_args = []
    for c in cands:
        cand_specs += [spec_ck, spec_cv]
        cand_args += [c, c]
    grid_spec = pltpu.PrefetchScalarGridSpec(
        num_scalar_prefetch=1,
        grid=(heads,),
        in_specs=[spec_q, spec_q, spec_q] + cand_specs + [spec_q,
                  pl.BlockSpec((rows, 1), lambda h, s: (0, 0)),
                  pl.BlockSpec((1, rows), lambda h, s: (0, 0))],
        out_specs=[spec_q, spec_q, spec_self, spec_pair, spec_pair, spec_pair],
    )
    pair_shape = jax.ShapeDtypeStruct((2, 2, rows, columns), jnp.bfloat16)
    out_shape = [
        jax.ShapeDtypeStruct((rows, columns), jnp.bfloat16),
        jax.ShapeDtypeStruct((rows, columns), jnp.bfloat16),
        jax.ShapeDtypeStruct((2, rows, columns), jnp.float32),
        pair_shape,
        pair_shape,
        pair_shape,
    ]
    kwargs = {}
    if INTERPRET is not None:
        kwargs["interpret"] = INTERPRET
    return pl.pallas_call(
        attn_kernel,
        grid_spec=grid_spec,
        out_shape=out_shape,
        compiler_params=pltpu.CompilerParams(vmem_limit_bytes=48 * 1024 * 1024),
        **kwargs,
    )(sel, queries, keys, values, *cand_args, grad_attn, shot_ids.reshape(rows, 1), shot_ids.reshape(1, rows))


def on_device(queries, keys, values, out_weight, cotangent, routes, shot_ids):
    seq_index = lax.axis_index("seq")
    parity = seq_index % 2
    grad_attn = fold_cotangent(cotangent, out_weight)
    own_kv = jnp.stack([keys, values])
    from_left2 = shifted(own_kv, "seq", 2)
    from_right2 = shifted(own_kv, "seq", -2)
    partner_own = partner_swap(own_kv, "seq")
    relay_to_odd = even_to_odd(from_right2, "seq")
    relay_to_even = odd_to_even(from_left2, "seq")
    partner_off = 1 - 2 * parity
    offs = (routes[seq_index] - seq_index).astype(jnp.int32)
    relay_idx = jnp.where(parity == 1, 2, 3)
    pick = jnp.where(offs == -2, 0, jnp.where(offs == 2, 4, jnp.where(offs == partner_off, 1, relay_idx)))
    sel = jnp.concatenate([pick.astype(jnp.int32), jnp.zeros((1,), jnp.int32), offs])
    cands = (from_left2, partner_own, relay_to_odd, relay_to_even, from_right2)
    attn, grad_q, self_term, pair_a, pair_b, far = attention(
        sel, queries, keys, values, cands, grad_attn, shot_ids
    )
    attn_out = project_out(attn, out_weight)
    got_a = even_to_odd(pair_a, "seq")
    got_b = odd_to_even(pair_b, "seq")
    up_plus = (far[1].astype(jnp.float32) + got_b[1].astype(jnp.float32)).astype(jnp.bfloat16)
    up_minus = (far[0].astype(jnp.float32) + got_a[1].astype(jnp.float32)).astype(jnp.bfloat16)
    got_from_left = shifted(up_plus, "seq", 2)
    got_from_right = shifted(up_minus, "seq", -2)
    total = (
        self_term
        + got_a[0].astype(jnp.float32)
        + got_b[0].astype(jnp.float32)
        + got_from_left.astype(jnp.float32)
        + got_from_right.astype(jnp.float32)
    )
    rounded = total.astype(jnp.bfloat16)
    return (attn_out, grad_q, rounded[0], rounded[1])


def solution(mesh):
    in_specs = (
        P("seq", "head"),
        P("seq", "head"),
        P("seq", "head"),
        P("head", None),
        P("seq", "head"),
        P(),
        P("seq"),
    )
    out_specs = (P("seq", "head"), P("seq", "head"), P("seq", "head"), P("seq", "head"))
    return jax.shard_map(
        on_device, mesh=mesh, in_specs=in_specs, out_specs=out_specs, check_vma=False
    )
```

```python
import jax
import jax.numpy as jnp
from jax import lax
from jax.experimental import pallas as pl
from jax.experimental.pallas import tpu as pltpu
from jax.sharding import PartitionSpec as P

HEAD_DIM = 128
BLOCK_LEN = 512
NEG_BIG = -1e30
INTERPRET = None


def shifted(block, axis, distance):
    devices = range(lax.axis_size(axis))
    route = [(i - distance, i) for i in devices if i - distance in devices]
    return lax.ppermute(block, axis, route)


def ring_shift(block, axis, distance):
    size = lax.axis_size(axis)
    return lax.ppermute(block, axis, [(i, (i + distance) % size) for i in range(size)])


def head_slice(array, group, width):
    return lax.dynamic_slice_in_dim(array, group * width, width, 1)


def fold_cotangent(cotangent, out_weight):
    groups = lax.axis_size("head")
    rows, width = cotangent.shape
    sent = jnp.broadcast_to(cotangent[None], (groups, rows, width))
    got = lax.all_to_all(sent, "head", 0, 0, tiled=True)
    nt = (((1,), (1,)), ((), ()))
    acc = None
    for group in range(groups):
        w_cols = out_weight[:, group * width:(group + 1) * width]
        part = lax.dot_general(got[group], w_cols, nt, preferred_element_type=jnp.float32)
        acc = part if acc is None else acc + part
    return acc.astype(jnp.bfloat16)


def project_out(attn, out_weight):
    groups = lax.axis_size("head")
    rows, width = attn.shape
    parts = jnp.stack([
        jnp.dot(attn, out_weight[:, c * width:(c + 1) * width], preferred_element_type=jnp.float32)
        .astype(jnp.bfloat16)
        for c in range(groups)
    ])
    got = lax.all_to_all(parts, "head", 0, 0, tiled=True).astype(jnp.float32)
    return got.sum(axis=0).astype(jnp.bfloat16)


def partner_swap(block, axis):
    size = lax.axis_size(axis)
    return lax.ppermute(block, axis, [(i, i ^ 1) for i in range(size)])


def even_to_odd(block, axis):
    size = lax.axis_size(axis)
    return lax.ppermute(block, axis, [(i, i + 1) for i in range(0, size - 1, 2)])


def odd_to_even(block, axis):
    size = lax.axis_size(axis)
    return lax.ppermute(block, axis, [(i, i - 1) for i in range(1, size, 2)])


def attn_kernel(sel_ref, q_ref, k0_ref, v0_ref, *refs):
    n_cand = 5
    cand_k = refs[0:2 * n_cand:2]
    cand_v = refs[1:2 * n_cand:2]
    g_ref, srow_ref, scol_ref, attn_ref, dq_ref, self_ref, pa_ref, pb_ref, far_ref = refs[2 * n_cand:]
    scale = HEAD_DIM ** (-0.5)
    d = HEAD_DIM
    h = pl.program_id(0)

    @pl.when(h == 0)
    def _():
        pa_ref[...] = jnp.zeros_like(pa_ref)
        pb_ref[...] = jnp.zeros_like(pb_ref)
        far_ref[...] = jnp.zeros_like(far_ref)

    def pick(cands, slot):
        idx = sel_ref[slot]
        out = cands[0][...]
        for c in range(1, n_cand):
            out = jnp.where(idx == c, cands[c][...], out)
        return out

    ks = [k0_ref[...], pick(cand_k, 0), pick(cand_k, 1)]
    vs = [v0_ref[...], pick(cand_v, 0), pick(cand_v, 1)]
    q = q_ref[...]
    g = g_ref[...]
    nt = (((1,), (1,)), ((), ()))
    tn = (((0,), (0,)), ((), ()))
    scores = [lax.dot_general(q, k, nt, preferred_element_type=jnp.float32) * scale for k in ks]
    visible = srow_ref[...] == scol_ref[...]
    scores[0] = jnp.where(visible, scores[0], NEG_BIG)
    top = jnp.max(scores[0], axis=1, keepdims=True)
    for s in scores[1:]:
        top = jnp.maximum(top, jnp.max(s, axis=1, keepdims=True))
    weights = [jnp.exp(s - top) for s in scores]
    weights[0] = jnp.where(visible, weights[0], 0.0)
    total = weights[0].sum(axis=1, keepdims=True)
    for w in weights[1:]:
        total = total + w.sum(axis=1, keepdims=True)
    inv = 1.0 / total
    probs = [w * inv for w in weights]
    low = [p.astype(jnp.bfloat16) for p in probs]
    acc = jnp.dot(low[0], vs[0], preferred_element_type=jnp.float32)
    for j in (1, 2):
        acc = acc + jnp.dot(low[j], vs[j], preferred_element_type=jnp.float32)
    attn = acc.astype(jnp.bfloat16)
    attn_ref[...] = attn
    gf = g.astype(jnp.float32)
    delta = jnp.sum(attn.astype(jnp.float32) * gf, axis=1, keepdims=True)
    dq = None
    cols = pl.ds(pl.multiple_of(h * d, d), d)
    for j in range(3):
        dp = lax.dot_general(g, vs[j], nt, preferred_element_type=jnp.float32)
        ds = (probs[j] * (dp - delta) * scale).astype(jnp.bfloat16)
        part = jnp.dot(ds, ks[j], preferred_element_type=jnp.float32)
        dq = part if dq is None else dq + part
        dk = lax.dot_general(ds, q, tn, preferred_element_type=jnp.float32)
        dv = lax.dot_general(low[j], g, tn, preferred_element_type=jnp.float32)
        if j == 0:
            self_ref[0] = dk
            self_ref[1] = dv
            continue
        dk = dk.astype(jnp.bfloat16)
        dv = dv.astype(jnp.bfloat16)
        off = sel_ref[2 + j]
        for value, dests in ((-2, ((far_ref, 0),)), (2, ((far_ref, 1),)),
                             (1, ((pa_ref, 0), (pb_ref, 1))), (-1, ((pa_ref, 1), (pb_ref, 0)))):
            @pl.when(off == value)
            def _():
                for ref, slot in dests:
                    ref[slot, 0, :, cols] = dk
                    ref[slot, 1, :, cols] = dv
    dq_ref[...] = dq.astype(jnp.bfloat16)


def attention(sel, queries, keys, values, cands, grad_attn, shot_ids):
    rows, columns = queries.shape
    heads = columns // HEAD_DIM
    d = HEAD_DIM
    spec_q = pl.BlockSpec((rows, d), lambda h, s: (0, h))
    spec_ck = pl.BlockSpec((None, rows, d), lambda h, s: (0, 0, h))
    spec_cv = pl.BlockSpec((None, rows, d), lambda h, s: (1, 0, h))
    spec_self = pl.BlockSpec((2, rows, d), lambda h, s: (0, 0, h))
    spec_pair = pl.BlockSpec((2, 2, rows, columns), lambda h, s: (0, 0, 0, 0))
    cand_specs = []
    cand_args = []
    for c in cands:
        cand_specs += [spec_ck, spec_cv]
        cand_args += [c, c]
    grid_spec = pltpu.PrefetchScalarGridSpec(
        num_scalar_prefetch=1,
        grid=(heads,),
        in_specs=[spec_q, spec_q, spec_q] + cand_specs + [spec_q,
                  pl.BlockSpec((rows, 1), lambda h, s: (0, 0)),
                  pl.BlockSpec((1, rows), lambda h, s: (0, 0))],
        out_specs=[spec_q, spec_q, spec_self, spec_pair, spec_pair, spec_pair],
    )
    pair_shape = jax.ShapeDtypeStruct((2, 2, rows, columns), jnp.bfloat16)
    out_shape = [
        jax.ShapeDtypeStruct((rows, columns), jnp.bfloat16),
        jax.ShapeDtypeStruct((rows, columns), jnp.bfloat16),
        jax.ShapeDtypeStruct((2, rows, columns), jnp.float32),
        pair_shape,
        pair_shape,
        pair_shape,
    ]
    kwargs = {}
    if INTERPRET is not None:
        kwargs["interpret"] = INTERPRET
    return pl.pallas_call(
        attn_kernel,
        grid_spec=grid_spec,
        out_shape=out_shape,
        compiler_params=pltpu.CompilerParams(vmem_limit_bytes=48 * 1024 * 1024),
        **kwargs,
    )(sel, queries, keys, values, *cand_args, grad_attn, shot_ids.reshape(rows, 1), shot_ids.reshape(1, rows))


def on_device(queries, keys, values, out_weight, cotangent, routes, shot_ids):
    seq_index = lax.axis_index("seq")
    parity = seq_index % 2
    grad_attn = fold_cotangent(cotangent, out_weight)
    own_kv = jnp.stack([keys, values])
    from_left2 = shifted(own_kv, "seq", 2)
    from_right2 = shifted(own_kv, "seq", -2)
    partner_own = partner_swap(own_kv, "seq")
    relay_to_odd = even_to_odd(from_right2, "seq")
    relay_to_even = odd_to_even(from_left2, "seq")
    partner_off = 1 - 2 * parity
    offs = (routes[seq_index] - seq_index).astype(jnp.int32)
    relay_idx = jnp.where(parity == 1, 2, 3)
    pick = jnp.where(offs == -2, 0, jnp.where(offs == 2, 4, jnp.where(offs == partner_off, 1, relay_idx)))
    sel = jnp.concatenate([pick.astype(jnp.int32), jnp.zeros((1,), jnp.int32), offs])
    cands = (from_left2, partner_own, relay_to_odd, relay_to_even, from_right2)
    attn, grad_q, self_term, pair_a, pair_b, far = attention(
        sel, queries, keys, values, cands, grad_attn, shot_ids
    )
    attn_out = project_out(attn, out_weight)
    got_a = even_to_odd(pair_a, "seq")
    got_b = odd_to_even(pair_b, "seq")
    up_plus = (far[1].astype(jnp.float32) + got_b[1].astype(jnp.float32)).astype(jnp.bfloat16)
    up_minus = (far[0].astype(jnp.float32) + got_a[1].astype(jnp.float32)).astype(jnp.bfloat16)
    got_from_left = shifted(up_plus, "seq", 2)
    got_from_right = shifted(up_minus, "seq", -2)
    total = (
        self_term
        + got_a[0].astype(jnp.float32)
        + got_b[0].astype(jnp.float32)
        + got_from_left.astype(jnp.float32)
        + got_from_right.astype(jnp.float32)
    )
    rounded = total.astype(jnp.bfloat16)
    return (attn_out, grad_q, rounded[0], rounded[1])


def solution(mesh):
    in_specs = (
        P("seq", "head"),
        P("seq", "head"),
        P("seq", "head"),
        P("head", None),
        P("seq", "head"),
        P(),
        P("seq"),
    )
    out_specs = (P("seq", "head"), P("seq", "head"), P("seq", "head"), P("seq", "head"))
    return jax.shard_map(
        on_device, mesh=mesh, in_specs=in_specs, out_specs=out_specs, check_vma=False
    )
```

```python
import jax
import jax.numpy as jnp
from jax import lax
from jax.experimental import pallas as pl
from jax.experimental.pallas import tpu as pltpu
from jax.sharding import PartitionSpec as P


HEAD_DIM = 128
NEG_BIG = -1e30
INTERPRET = None


def shifted(block, axis, distance):
    devices = range(lax.axis_size(axis))
    route = [(i - distance, i) for i in devices if i - distance in devices]
    return lax.ppermute(block, axis, route)


def ring_shift(block, axis, distance):
    size = lax.axis_size(axis)
    return lax.ppermute(block, axis, [(i, (i + distance) % size) for i in range(size)])


def head_slice(array, group, width):
    return lax.dynamic_slice_in_dim(array, group * width, width, 1)


def fold_cotangent(cotangent, out_weight):
    groups = lax.axis_size("head")
    me = lax.axis_index("head")
    rows, width = cotangent.shape
    half = rows // 2
    from_prev = ring_shift(cotangent, "head", 1)
    from_next = ring_shift(cotangent, "head", -1)
    far_a = ring_shift(cotangent[:half], "head", 2)
    far_b = ring_shift(cotangent[half:], "head", -2)
    far = jnp.concatenate([far_a, far_b], axis=0)
    nt = (((1,), (1,)), ((), ()))
    acc = None
    for piece, group in ((cotangent, me), (from_prev, me - 1), (from_next, me + 1), (far, me + 2)):
        w_cols = head_slice(out_weight, group % groups, width)
        part = lax.dot_general(piece, w_cols, nt, preferred_element_type=jnp.float32)
        acc = part if acc is None else acc + part
    return acc.astype(jnp.bfloat16)


def project_out(attn, out_weight):
    groups = lax.axis_size("head")
    me = lax.axis_index("head")
    rows, width = attn.shape
    half = rows // 2

    def part(group):
        w_cols = head_slice(out_weight, group % groups, width)
        return jnp.dot(attn, w_cols, preferred_element_type=jnp.float32).astype(jnp.bfloat16)

    far = part(me + 2)
    near_up = part(me + 1)
    near_down = part(me - 1)
    got_a = ring_shift(far[:half], "head", 2)
    got_b = ring_shift(far[half:], "head", -2)
    from_prev = ring_shift(near_up, "head", 1)
    from_next = ring_shift(near_down, "head", -1)
    total = (
        jnp.dot(attn, head_slice(out_weight, me, width), preferred_element_type=jnp.float32)
        + from_prev.astype(jnp.float32)
        + from_next.astype(jnp.float32)
        + jnp.concatenate([got_a, got_b], axis=0).astype(jnp.float32)
    )
    return total.astype(jnp.bfloat16)


def partner_swap(block, axis):
    size = lax.axis_size(axis)
    return lax.ppermute(block, axis, [(i, i ^ 1) for i in range(size)])


def even_to_odd(block, axis):
    size = lax.axis_size(axis)
    return lax.ppermute(block, axis, [(i, i + 1) for i in range(0, size - 1, 2)])


def odd_to_even(block, axis):
    size = lax.axis_size(axis)
    return lax.ppermute(block, axis, [(i, i - 1) for i in range(1, size, 2)])


def attn_kernel(sel_ref, q_ref, k0_ref, v0_ref, *refs):
    n_cand = 5
    cand_k = refs[0:2 * n_cand:2]
    cand_v = refs[1:2 * n_cand:2]
    g_ref, srow_ref, scol_ref, attn_ref, dq_ref, self_ref, pa_ref, pb_ref, far_ref = refs[2 * n_cand:]
    scale = HEAD_DIM ** (-0.5)
    d = HEAD_DIM
    h = pl.program_id(0)

    @pl.when(h == 0)
    def _():
        pa_ref[...] = jnp.zeros_like(pa_ref)
        pb_ref[...] = jnp.zeros_like(pb_ref)
        far_ref[...] = jnp.zeros_like(far_ref)

    def pick(cands, slot):
        idx = sel_ref[slot]
        out = cands[0][...]
        for c in range(1, n_cand):
            out = jnp.where(idx == c, cands[c][...], out)
        return out

    ks = [k0_ref[...], pick(cand_k, 0), pick(cand_k, 1)]
    vs = [v0_ref[...], pick(cand_v, 0), pick(cand_v, 1)]
    q = q_ref[...]
    g = g_ref[...]
    nt = (((1,), (1,)), ((), ()))
    tn = (((0,), (0,)), ((), ()))
    scores = [lax.dot_general(q, k, nt, preferred_element_type=jnp.float32) * scale for k in ks]
    visible = srow_ref[...] == scol_ref[...]
    scores[0] = jnp.where(visible, scores[0], NEG_BIG)
    top = jnp.max(scores[0], axis=1, keepdims=True)
    for s in scores[1:]:
        top = jnp.maximum(top, jnp.max(s, axis=1, keepdims=True))
    weights = [jnp.exp(s - top) for s in scores]
    weights[0] = jnp.where(visible, weights[0], 0.0)
    total = weights[0].sum(axis=1, keepdims=True)
    for w in weights[1:]:
        total = total + w.sum(axis=1, keepdims=True)
    inv = 1.0 / total
    probs = [w * inv for w in weights]
    low = [p.astype(jnp.bfloat16) for p in probs]
    acc = jnp.dot(low[0], vs[0], preferred_element_type=jnp.float32)
    for j in (1, 2):
        acc = acc + jnp.dot(low[j], vs[j], preferred_element_type=jnp.float32)
    attn = acc.astype(jnp.bfloat16)
    attn_ref[...] = attn
    gf = g.astype(jnp.float32)
    delta = jnp.sum(attn.astype(jnp.float32) * gf, axis=1, keepdims=True)
    dq = None
    cols = pl.ds(pl.multiple_of(h * d, d), d)
    for j in range(3):
        dp = lax.dot_general(g, vs[j], nt, preferred_element_type=jnp.float32)
        ds = (probs[j] * (dp - delta) * scale).astype(jnp.bfloat16)
        part = jnp.dot(ds, ks[j], preferred_element_type=jnp.float32)
        dq = part if dq is None else dq + part
        dk = lax.dot_general(ds, q, tn, preferred_element_type=jnp.float32)
        dv = lax.dot_general(low[j], g, tn, preferred_element_type=jnp.float32)
        if j == 0:
            self_ref[0] = dk
            self_ref[1] = dv
            continue
        dk = dk.astype(jnp.bfloat16)
        dv = dv.astype(jnp.bfloat16)
        off = sel_ref[2 + j]
        for value, dests in ((-2, ((far_ref, 0),)), (2, ((far_ref, 1),)),
                             (1, ((pa_ref, 0), (pb_ref, 1))), (-1, ((pa_ref, 1), (pb_ref, 0)))):
            @pl.when(off == value)
            def _():
                for ref, slot in dests:
                    ref[slot, 0, :, cols] = dk
                    ref[slot, 1, :, cols] = dv
    dq_ref[...] = dq.astype(jnp.bfloat16)


def attention(sel, queries, keys, values, cands, grad_attn, shot_ids):
    rows, columns = queries.shape
    heads = columns // HEAD_DIM
    d = HEAD_DIM
    spec_q = pl.BlockSpec((rows, d), lambda h, s: (0, h))
    spec_ck = pl.BlockSpec((None, rows, d), lambda h, s: (0, 0, h))
    spec_cv = pl.BlockSpec((None, rows, d), lambda h, s: (1, 0, h))
    spec_self = pl.BlockSpec((2, rows, d), lambda h, s: (0, 0, h))
    spec_pair = pl.BlockSpec((2, 2, rows, columns), lambda h, s: (0, 0, 0, 0))
    cand_specs = []
    cand_args = []
    for c in cands:
        cand_specs += [spec_ck, spec_cv]
        cand_args += [c, c]
    grid_spec = pltpu.PrefetchScalarGridSpec(
        num_scalar_prefetch=1,
        grid=(heads,),
        in_specs=[spec_q, spec_q, spec_q] + cand_specs + [spec_q,
                  pl.BlockSpec((rows, 1), lambda h, s: (0, 0)),
                  pl.BlockSpec((1, rows), lambda h, s: (0, 0))],
        out_specs=[spec_q, spec_q, spec_self, spec_pair, spec_pair, spec_pair],
    )
    pair_shape = jax.ShapeDtypeStruct((2, 2, rows, columns), jnp.bfloat16)
    out_shape = [
        jax.ShapeDtypeStruct((rows, columns), jnp.bfloat16),
        jax.ShapeDtypeStruct((rows, columns), jnp.bfloat16),
        jax.ShapeDtypeStruct((2, rows, columns), jnp.float32),
        pair_shape,
        pair_shape,
        pair_shape,
    ]
    kwargs = {}
    if INTERPRET is not None:
        kwargs["interpret"] = INTERPRET
    return pl.pallas_call(
        attn_kernel,
        grid_spec=grid_spec,
        out_shape=out_shape,
        compiler_params=pltpu.CompilerParams(vmem_limit_bytes=48 * 1024 * 1024),
        **kwargs,
    )(sel, queries, keys, values, *cand_args, grad_attn, shot_ids.reshape(rows, 1), shot_ids.reshape(1, rows))


def on_device(queries, keys, values, out_weight, cotangent, routes, shot_ids):
    seq_index = lax.axis_index("seq")
    parity = seq_index % 2
    grad_attn = fold_cotangent(cotangent, out_weight)
    own_kv = jnp.stack([keys, values])
    from_left2 = shifted(own_kv, "seq", 2)
    from_right2 = shifted(own_kv, "seq", -2)
    partner_own = partner_swap(own_kv, "seq")
    relay_to_odd = even_to_odd(from_right2, "seq")
    relay_to_even = odd_to_even(from_left2, "seq")
    partner_off = 1 - 2 * parity
    offs = (routes[seq_index] - seq_index).astype(jnp.int32)
    relay_idx = jnp.where(parity == 1, 2, 3)
    pick = jnp.where(offs == -2, 0, jnp.where(offs == 2, 4, jnp.where(offs == partner_off, 1, relay_idx)))
    sel = jnp.concatenate([pick.astype(jnp.int32), jnp.zeros((1,), jnp.int32), offs])
    cands = (from_left2, partner_own, relay_to_odd, relay_to_even, from_right2)
    attn, grad_q, self_term, pair_a, pair_b, far = attention(
        sel, queries, keys, values, cands, grad_attn, shot_ids
    )
    attn_out = project_out(attn, out_weight)
    got_a = even_to_odd(pair_a, "seq")
    got_b = odd_to_even(pair_b, "seq")
    up_plus = (far[1].astype(jnp.float32) + got_b[1].astype(jnp.float32)).astype(jnp.bfloat16)
    up_minus = (far[0].astype(jnp.float32) + got_a[1].astype(jnp.float32)).astype(jnp.bfloat16)
    got_from_left = shifted(up_plus, "seq", 2)
    got_from_right = shifted(up_minus, "seq", -2)
    total = (
        self_term
        + got_a[0].astype(jnp.float32)
        + got_b[0].astype(jnp.float32)
        + got_from_left.astype(jnp.float32)
        + got_from_right.astype(jnp.float32)
    )
    rounded = total.astype(jnp.bfloat16)
    return (attn_out, grad_q, rounded[0], rounded[1])


def solution(mesh):
    in_specs = (
        P("seq", "head"),
        P("seq", "head"),
        P("seq", "head"),
        P("head", None),
        P("seq", "head"),
        P(),
        P("seq"),
    )
    out_specs = (P("seq", "head"), P("seq", "head"), P("seq", "head"), P("seq", "head"))

    return jax.shard_map(on_device, mesh=mesh, in_specs=in_specs, out_specs=out_specs, check_vma=False)
```

```python
import jax
import jax.numpy as jnp
from jax import lax
from jax.experimental import pallas as pl
from jax.experimental.pallas import tpu as pltpu
from jax.sharding import PartitionSpec as P


HEAD_DIM = 128
NEG_BIG = -1e30
INTERPRET = None


def shifted(block, axis, distance):
    devices = range(lax.axis_size(axis))
    route = [(i - distance, i) for i in devices if i - distance in devices]
    return lax.ppermute(block, axis, route)


def ring_shift(block, axis, distance):
    size = lax.axis_size(axis)
    return lax.ppermute(block, axis, [(i, (i + distance) % size) for i in range(size)])


def head_slice(array, group, width):
    return lax.dynamic_slice_in_dim(array, group * width, width, 1)


def fold_cotangent(cotangent, out_weight):
    groups = lax.axis_size("head")
    me = lax.axis_index("head")
    rows, width = cotangent.shape
    half = rows // 2
    from_prev = ring_shift(cotangent, "head", 1)
    from_next = ring_shift(cotangent, "head", -1)
    far_a = ring_shift(cotangent[:half], "head", 2)
    far_b = ring_shift(cotangent[half:], "head", -2)
    far = jnp.concatenate([far_a, far_b], axis=0)
    nt = (((1,), (1,)), ((), ()))
    acc = None
    for piece, group in ((cotangent, me), (from_prev, me - 1), (from_next, me + 1), (far, me + 2)):
        w_cols = head_slice(out_weight, group % groups, width)
        part = lax.dot_general(piece, w_cols, nt, preferred_element_type=jnp.float32)
        acc = part if acc is None else acc + part
    return acc.astype(jnp.bfloat16)


def project_out(attn, out_weight):
    groups = lax.axis_size("head")
    me = lax.axis_index("head")
    rows, width = attn.shape
    half = rows // 2

    def part(group):
        w_cols = head_slice(out_weight, group % groups, width)
        return jnp.dot(attn, w_cols, preferred_element_type=jnp.float32).astype(jnp.bfloat16)

    far = part(me + 2)
    near_up = part(me + 1)
    near_down = part(me - 1)
    got_a = ring_shift(far[:half], "head", 2)
    got_b = ring_shift(far[half:], "head", -2)
    from_prev = ring_shift(near_up, "head", 1)
    from_next = ring_shift(near_down, "head", -1)
    total = (
        jnp.dot(attn, head_slice(out_weight, me, width), preferred_element_type=jnp.float32)
        + from_prev.astype(jnp.float32)
        + from_next.astype(jnp.float32)
        + jnp.concatenate([got_a, got_b], axis=0).astype(jnp.float32)
    )
    return total.astype(jnp.bfloat16)


def partner_swap(block, axis):
    size = lax.axis_size(axis)
    return lax.ppermute(block, axis, [(i, i ^ 1) for i in range(size)])


def even_to_odd(block, axis):
    size = lax.axis_size(axis)
    return lax.ppermute(block, axis, [(i, i + 1) for i in range(0, size - 1, 2)])


def odd_to_even(block, axis):
    size = lax.axis_size(axis)
    return lax.ppermute(block, axis, [(i, i - 1) for i in range(1, size, 2)])


def attn_kernel(sel_ref, q_ref, k0_ref, v0_ref, *refs):
    n_cand = 5
    cand_k = refs[0:2 * n_cand:2]
    cand_v = refs[1:2 * n_cand:2]
    g_ref, srow_ref, scol_ref, attn_ref, dq_ref, self_ref, terms_ref = refs[2 * n_cand:]
    scale = HEAD_DIM ** (-0.5)

    def pick(cands, slot):
        idx = sel_ref[slot]
        out = cands[0][...]
        for c in range(1, n_cand):
            out = jnp.where(idx == c, cands[c][...], out)
        return out

    ks = [k0_ref[...], pick(cand_k, 0), pick(cand_k, 1)]
    vs = [v0_ref[...], pick(cand_v, 0), pick(cand_v, 1)]
    q = q_ref[...]
    g = g_ref[...]
    nt = (((1,), (1,)), ((), ()))
    tn = (((0,), (0,)), ((), ()))
    scores = [lax.dot_general(q, k, nt, preferred_element_type=jnp.float32) * scale for k in ks]
    visible = srow_ref[...] == scol_ref[...]
    scores[0] = jnp.where(visible, scores[0], NEG_BIG)
    top = jnp.max(scores[0], axis=1, keepdims=True)
    for s in scores[1:]:
        top = jnp.maximum(top, jnp.max(s, axis=1, keepdims=True))
    weights = [jnp.exp(s - top) for s in scores]
    weights[0] = jnp.where(visible, weights[0], 0.0)
    total = weights[0].sum(axis=1, keepdims=True)
    for w in weights[1:]:
        total = total + w.sum(axis=1, keepdims=True)
    inv = 1.0 / total
    probs = [w * inv for w in weights]
    low = [p.astype(jnp.bfloat16) for p in probs]
    acc = jnp.dot(low[0], vs[0], preferred_element_type=jnp.float32)
    for j in (1, 2):
        acc = acc + jnp.dot(low[j], vs[j], preferred_element_type=jnp.float32)
    attn = acc.astype(jnp.bfloat16)
    attn_ref[...] = attn
    gf = g.astype(jnp.float32)
    delta = jnp.sum(attn.astype(jnp.float32) * gf, axis=1, keepdims=True)
    dq = None
    routed = []
    for j in range(3):
        dp = lax.dot_general(g, vs[j], nt, preferred_element_type=jnp.float32)
        ds = (probs[j] * (dp - delta) * scale).astype(jnp.bfloat16)
        part = jnp.dot(ds, ks[j], preferred_element_type=jnp.float32)
        dq = part if dq is None else dq + part
        dk = lax.dot_general(ds, q, tn, preferred_element_type=jnp.float32)
        dv = lax.dot_general(low[j], g, tn, preferred_element_type=jnp.float32)
        if j == 0:
            self_ref[0] = dk
            self_ref[1] = dv
        else:
            routed.append((sel_ref[2 + j], dk.astype(jnp.bfloat16), dv.astype(jnp.bfloat16)))
    (off1, dk1, dv1), (off2, dk2, dv2) = routed
    zero = jnp.zeros_like(dk1)
    for slot, value in enumerate((-2, -1, 1, 2)):
        terms_ref[slot, 0] = jnp.where(off1 == value, dk1, jnp.where(off2 == value, dk2, zero))
        terms_ref[slot, 1] = jnp.where(off1 == value, dv1, jnp.where(off2 == value, dv2, zero))
    dq_ref[...] = dq.astype(jnp.bfloat16)


def attention(sel, queries, keys, values, cands, grad_attn, shot_ids):
    rows, columns = queries.shape
    heads = columns // HEAD_DIM
    d = HEAD_DIM
    spec_q = pl.BlockSpec((rows, d), lambda h, s: (0, h))
    spec_ck = pl.BlockSpec((None, rows, d), lambda h, s: (0, 0, h))
    spec_cv = pl.BlockSpec((None, rows, d), lambda h, s: (1, 0, h))
    spec_self = pl.BlockSpec((2, rows, d), lambda h, s: (0, 0, h))
    spec_terms = pl.BlockSpec((4, 2, rows, d), lambda h, s: (0, 0, 0, h))
    cand_specs = []
    cand_args = []
    for c in cands:
        cand_specs += [spec_ck, spec_cv]
        cand_args += [c, c]
    grid_spec = pltpu.PrefetchScalarGridSpec(
        num_scalar_prefetch=1,
        grid=(heads,),
        in_specs=[spec_q, spec_q, spec_q] + cand_specs + [spec_q,
                  pl.BlockSpec((rows, 1), lambda h, s: (0, 0)),
                  pl.BlockSpec((1, rows), lambda h, s: (0, 0))],
        out_specs=[spec_q, spec_q, spec_self, spec_terms],
    )
    out_shape = [
        jax.ShapeDtypeStruct((rows, columns), jnp.bfloat16),
        jax.ShapeDtypeStruct((rows, columns), jnp.bfloat16),
        jax.ShapeDtypeStruct((2, rows, columns), jnp.float32),
        jax.ShapeDtypeStruct((4, 2, rows, columns), jnp.bfloat16),
    ]
    kwargs = {}
    if INTERPRET is not None:
        kwargs["interpret"] = INTERPRET
    return pl.pallas_call(
        attn_kernel,
        grid_spec=grid_spec,
        out_shape=out_shape,
        compiler_params=pltpu.CompilerParams(vmem_limit_bytes=48 * 1024 * 1024),
        **kwargs,
    )(sel, queries, keys, values, *cand_args, grad_attn, shot_ids.reshape(rows, 1), shot_ids.reshape(1, rows))


def on_device(queries, keys, values, out_weight, cotangent, routes, shot_ids):
    seq_index = lax.axis_index("seq")
    parity = seq_index % 2
    grad_attn = fold_cotangent(cotangent, out_weight)
    own_kv = jnp.stack([keys, values])
    from_left2 = shifted(own_kv, "seq", 2)
    from_right2 = shifted(own_kv, "seq", -2)
    partner_own = partner_swap(own_kv, "seq")
    relay_to_odd = even_to_odd(from_right2, "seq")
    relay_to_even = odd_to_even(from_left2, "seq")
    partner_off = 1 - 2 * parity
    offs = (routes[seq_index] - seq_index).astype(jnp.int32)
    relay_idx = jnp.where(parity == 1, 2, 3)
    pick = jnp.where(offs == -2, 0, jnp.where(offs == 2, 4, jnp.where(offs == partner_off, 1, relay_idx)))
    sel = jnp.concatenate([pick.astype(jnp.int32), jnp.zeros((1,), jnp.int32), offs])
    cands = (from_left2, partner_own, relay_to_odd, relay_to_even, from_right2)
    attn, grad_q, self_term, terms = attention(sel, queries, keys, values, cands, grad_attn, shot_ids)
    attn_out = project_out(attn, out_weight)
    near = terms[1:3]
    got_a = even_to_odd(near, "seq")
    got_b = odd_to_even(near, "seq")
    up_plus = (terms[3].astype(jnp.float32) + got_b[1].astype(jnp.float32)).astype(jnp.bfloat16)
    up_minus = (terms[0].astype(jnp.float32) + got_a[0].astype(jnp.float32)).astype(jnp.bfloat16)
    got_from_left = shifted(up_plus, "seq", 2)
    got_from_right = shifted(up_minus, "seq", -2)
    total = (
        self_term
        + got_a[1].astype(jnp.float32)
        + got_b[0].astype(jnp.float32)
        + got_from_left.astype(jnp.float32)
        + got_from_right.astype(jnp.float32)
    )
    rounded = total.astype(jnp.bfloat16)
    return (attn_out, grad_q, rounded[0], rounded[1])


def solution(mesh):
    in_specs = (
        P("seq", "head"),
        P("seq", "head"),
        P("seq", "head"),
        P("head", None),
        P("seq", "head"),
        P(),
        P("seq"),
    )
    out_specs = (P("seq", "head"), P("seq", "head"), P("seq", "head"), P("seq", "head"))

    return jax.shard_map(on_device, mesh=mesh, in_specs=in_specs, out_specs=out_specs, check_vma=False)
```

```python
import jax
import jax.numpy as jnp
from jax import lax
from jax.experimental import pallas as pl
from jax.experimental.pallas import tpu as pltpu
from jax.sharding import PartitionSpec as P


HEAD_DIM = 128
NEG_BIG = -1e30
INTERPRET = None


def shifted(block, axis, distance):
    devices = range(lax.axis_size(axis))
    route = [(i - distance, i) for i in devices if i - distance in devices]
    return lax.ppermute(block, axis, route)


def ring_shift(block, axis, distance):
    size = lax.axis_size(axis)
    return lax.ppermute(block, axis, [(i, (i + distance) % size) for i in range(size)])


def head_slice(array, group, width):
    return lax.dynamic_slice_in_dim(array, group * width, width, 1)


def fold_cotangent(cotangent, out_weight):
    groups = lax.axis_size("head")
    me = lax.axis_index("head")
    rows, width = cotangent.shape
    half = rows // 2
    from_prev = ring_shift(cotangent, "head", 1)
    from_next = ring_shift(cotangent, "head", -1)
    far_a = ring_shift(cotangent[:half], "head", 2)
    far_b = ring_shift(cotangent[half:], "head", -2)
    far = jnp.concatenate([far_a, far_b], axis=0)
    nt = (((1,), (1,)), ((), ()))
    acc = None
    for piece, group in ((cotangent, me), (from_prev, me - 1), (from_next, me + 1), (far, me + 2)):
        w_cols = head_slice(out_weight, group % groups, width)
        part = lax.dot_general(piece, w_cols, nt, preferred_element_type=jnp.float32)
        acc = part if acc is None else acc + part
    return acc.astype(jnp.bfloat16)


def project_out(attn, out_weight):
    groups = lax.axis_size("head")
    me = lax.axis_index("head")
    rows, width = attn.shape
    half = rows // 2

    def part(group):
        w_cols = head_slice(out_weight, group % groups, width)
        return jnp.dot(attn, w_cols, preferred_element_type=jnp.float32).astype(jnp.bfloat16)

    far = part(me + 2)
    near_up = part(me + 1)
    near_down = part(me - 1)
    got_a = ring_shift(far[:half], "head", 2)
    got_b = ring_shift(far[half:], "head", -2)
    from_prev = ring_shift(near_up, "head", 1)
    from_next = ring_shift(near_down, "head", -1)
    total = (
        jnp.dot(attn, head_slice(out_weight, me, width), preferred_element_type=jnp.float32)
        + from_prev.astype(jnp.float32)
        + from_next.astype(jnp.float32)
        + jnp.concatenate([got_a, got_b], axis=0).astype(jnp.float32)
    )
    return total.astype(jnp.bfloat16)


def partner_swap(block, axis):
    size = lax.axis_size(axis)
    return lax.ppermute(block, axis, [(i, i ^ 1) for i in range(size)])


def even_to_odd(block, axis):
    size = lax.axis_size(axis)
    return lax.ppermute(block, axis, [(i, i + 1) for i in range(0, size - 1, 2)])


def odd_to_even(block, axis):
    size = lax.axis_size(axis)
    return lax.ppermute(block, axis, [(i, i - 1) for i in range(1, size, 2)])


def attn_kernel(sel_ref, q_ref, k0_ref, v0_ref, *refs):
    n_cand = 5
    cand_k = refs[0:2 * n_cand:2]
    cand_v = refs[1:2 * n_cand:2]
    g_ref, srow_ref, scol_ref, attn_ref, dq_ref, self_ref, near_ref, far_ref = refs[2 * n_cand:]
    scale = HEAD_DIM ** (-0.5)

    def pick(cands, slot):
        idx = sel_ref[slot]
        out = cands[0][...]
        for c in range(1, n_cand):
            out = jnp.where(idx == c, cands[c][...], out)
        return out

    ks = [k0_ref[...], pick(cand_k, 0), pick(cand_k, 1)]
    vs = [v0_ref[...], pick(cand_v, 0), pick(cand_v, 1)]
    q = q_ref[...]
    g = g_ref[...]
    nt = (((1,), (1,)), ((), ()))
    tn = (((0,), (0,)), ((), ()))
    scores = [lax.dot_general(q, k, nt, preferred_element_type=jnp.float32) * scale for k in ks]
    visible = srow_ref[...] == scol_ref[...]
    scores[0] = jnp.where(visible, scores[0], NEG_BIG)
    top = jnp.max(scores[0], axis=1, keepdims=True)
    for s in scores[1:]:
        top = jnp.maximum(top, jnp.max(s, axis=1, keepdims=True))
    weights = [jnp.exp(s - top) for s in scores]
    weights[0] = jnp.where(visible, weights[0], 0.0)
    total = weights[0].sum(axis=1, keepdims=True)
    for w in weights[1:]:
        total = total + w.sum(axis=1, keepdims=True)
    inv = 1.0 / total
    probs = [w * inv for w in weights]
    low = [p.astype(jnp.bfloat16) for p in probs]
    acc = jnp.dot(low[0], vs[0], preferred_element_type=jnp.float32)
    for j in (1, 2):
        acc = acc + jnp.dot(low[j], vs[j], preferred_element_type=jnp.float32)
    attn = acc.astype(jnp.bfloat16)
    attn_ref[...] = attn
    gf = g.astype(jnp.float32)
    delta = jnp.sum(attn.astype(jnp.float32) * gf, axis=1, keepdims=True)
    dq = None
    routed = []
    for j in range(3):
        dp = lax.dot_general(g, vs[j], nt, preferred_element_type=jnp.float32)
        ds = (probs[j] * (dp - delta) * scale).astype(jnp.bfloat16)
        part = jnp.dot(ds, ks[j], preferred_element_type=jnp.float32)
        dq = part if dq is None else dq + part
        dk = lax.dot_general(ds, q, tn, preferred_element_type=jnp.float32)
        dv = lax.dot_general(low[j], g, tn, preferred_element_type=jnp.float32)
        if j == 0:
            self_ref[0] = dk
            self_ref[1] = dv
        else:
            routed.append((sel_ref[2 + j], dk.astype(jnp.bfloat16), dv.astype(jnp.bfloat16)))
    (off1, dk1, dv1), (off2, dk2, dv2) = routed
    zero = jnp.zeros_like(dk1)
    for ref, slot, value in ((far_ref, 0, -2), (near_ref, 0, -1), (near_ref, 1, 1), (far_ref, 1, 2)):
        ref[slot, 0] = jnp.where(off1 == value, dk1, jnp.where(off2 == value, dk2, zero))
        ref[slot, 1] = jnp.where(off1 == value, dv1, jnp.where(off2 == value, dv2, zero))
    dq_ref[...] = dq.astype(jnp.bfloat16)


def attention(sel, queries, keys, values, cands, grad_attn, shot_ids):
    rows, columns = queries.shape
    heads = columns // HEAD_DIM
    d = HEAD_DIM
    spec_q = pl.BlockSpec((rows, d), lambda h, s: (0, h))
    spec_ck = pl.BlockSpec((None, rows, d), lambda h, s: (0, 0, h))
    spec_cv = pl.BlockSpec((None, rows, d), lambda h, s: (1, 0, h))
    spec_self = pl.BlockSpec((2, rows, d), lambda h, s: (0, 0, h))
    spec_terms = pl.BlockSpec((2, 2, rows, d), lambda h, s: (0, 0, 0, h))
    cand_specs = []
    cand_args = []
    for c in cands:
        cand_specs += [spec_ck, spec_cv]
        cand_args += [c, c]
    grid_spec = pltpu.PrefetchScalarGridSpec(
        num_scalar_prefetch=1,
        grid=(heads,),
        in_specs=[spec_q, spec_q, spec_q] + cand_specs + [spec_q,
                  pl.BlockSpec((rows, 1), lambda h, s: (0, 0)),
                  pl.BlockSpec((1, rows), lambda h, s: (0, 0))],
        out_specs=[spec_q, spec_q, spec_self, spec_terms, spec_terms],
    )
    out_shape = [
        jax.ShapeDtypeStruct((rows, columns), jnp.bfloat16),
        jax.ShapeDtypeStruct((rows, columns), jnp.bfloat16),
        jax.ShapeDtypeStruct((2, rows, columns), jnp.float32),
        jax.ShapeDtypeStruct((2, 2, rows, columns), jnp.bfloat16),
        jax.ShapeDtypeStruct((2, 2, rows, columns), jnp.bfloat16),
    ]
    kwargs = {}
    if INTERPRET is not None:
        kwargs["interpret"] = INTERPRET
    return pl.pallas_call(
        attn_kernel,
        grid_spec=grid_spec,
        out_shape=out_shape,
        compiler_params=pltpu.CompilerParams(vmem_limit_bytes=48 * 1024 * 1024),
        **kwargs,
    )(sel, queries, keys, values, *cand_args, grad_attn, shot_ids.reshape(rows, 1), shot_ids.reshape(1, rows))


def on_device(queries, keys, values, out_weight, cotangent, routes, shot_ids):
    seq_index = lax.axis_index("seq")
    parity = seq_index % 2
    grad_attn = fold_cotangent(cotangent, out_weight)
    own_kv = jnp.stack([keys, values])
    from_left2 = shifted(own_kv, "seq", 2)
    from_right2 = shifted(own_kv, "seq", -2)
    partner_own = partner_swap(own_kv, "seq")
    relay_to_odd = even_to_odd(from_right2, "seq")
    relay_to_even = odd_to_even(from_left2, "seq")
    partner_off = 1 - 2 * parity
    offs = (routes[seq_index] - seq_index).astype(jnp.int32)
    relay_idx = jnp.where(parity == 1, 2, 3)
    pick = jnp.where(offs == -2, 0, jnp.where(offs == 2, 4, jnp.where(offs == partner_off, 1, relay_idx)))
    sel = jnp.concatenate([pick.astype(jnp.int32), jnp.zeros((1,), jnp.int32), offs])
    cands = (from_left2, partner_own, relay_to_odd, relay_to_even, from_right2)
    attn, grad_q, self_term, near, far = attention(sel, queries, keys, values, cands, grad_attn, shot_ids)
    attn_out = project_out(attn, out_weight)
    got_a = even_to_odd(near, "seq")
    got_b = odd_to_even(near, "seq")
    up_plus = (far[1].astype(jnp.float32) + got_b[1].astype(jnp.float32)).astype(jnp.bfloat16)
    up_minus = (far[0].astype(jnp.float32) + got_a[0].astype(jnp.float32)).astype(jnp.bfloat16)
    got_from_left = shifted(up_plus, "seq", 2)
    got_from_right = shifted(up_minus, "seq", -2)
    total = (
        self_term
        + got_a[1].astype(jnp.float32)
        + got_b[0].astype(jnp.float32)
        + got_from_left.astype(jnp.float32)
        + got_from_right.astype(jnp.float32)
    )
    rounded = total.astype(jnp.bfloat16)
    return (attn_out, grad_q, rounded[0], rounded[1])


def solution(mesh):
    in_specs = (
        P("seq", "head"),
        P("seq", "head"),
        P("seq", "head"),
        P("head", None),
        P("seq", "head"),
        P(),
        P("seq"),
    )
    out_specs = (P("seq", "head"), P("seq", "head"), P("seq", "head"), P("seq", "head"))

    return jax.shard_map(on_device, mesh=mesh, in_specs=in_specs, out_specs=out_specs, check_vma=False)
```

```python
import jax
import jax.numpy as jnp
from jax import lax
from jax.experimental import pallas as pl
from jax.experimental.pallas import tpu as pltpu
from jax.sharding import PartitionSpec as P


HEAD_DIM = 128
NEG_BIG = -1e30
INTERPRET = None


def shifted(block, axis, distance):
    devices = range(lax.axis_size(axis))
    route = [(i - distance, i) for i in devices if i - distance in devices]
    return lax.ppermute(block, axis, route)


def ring_shift(block, axis, distance):
    size = lax.axis_size(axis)
    return lax.ppermute(block, axis, [(i, (i + distance) % size) for i in range(size)])


def head_slice(array, group, width):
    return lax.dynamic_slice_in_dim(array, group * width, width, 1)


def fold_cotangent(cotangent, out_weight):
    groups = lax.axis_size("head")
    me = lax.axis_index("head")
    rows, width = cotangent.shape
    half = rows // 2
    from_prev = ring_shift(cotangent, "head", 1)
    from_next = ring_shift(cotangent, "head", -1)
    far_a = ring_shift(cotangent[:half], "head", 2)
    far_b = ring_shift(cotangent[half:], "head", -2)
    far = jnp.concatenate([far_a, far_b], axis=0)
    nt = (((1,), (1,)), ((), ()))
    acc = None
    for piece, group in ((cotangent, me), (from_prev, me - 1), (from_next, me + 1), (far, me + 2)):
        w_cols = head_slice(out_weight, group % groups, width)
        part = lax.dot_general(piece, w_cols, nt, preferred_element_type=jnp.float32)
        acc = part if acc is None else acc + part
    return acc.astype(jnp.bfloat16)


def project_out(attn, out_weight):
    groups = lax.axis_size("head")
    me = lax.axis_index("head")
    rows, width = attn.shape
    half = rows // 2

    def part(group):
        w_cols = head_slice(out_weight, group % groups, width)
        return jnp.dot(attn, w_cols, preferred_element_type=jnp.float32).astype(jnp.bfloat16)

    far = part(me + 2)
    near_up = part(me + 1)
    near_down = part(me - 1)
    got_a = ring_shift(far[:half], "head", 2)
    got_b = ring_shift(far[half:], "head", -2)
    from_prev = ring_shift(near_up, "head", 1)
    from_next = ring_shift(near_down, "head", -1)
    total = (
        jnp.dot(attn, head_slice(out_weight, me, width), preferred_element_type=jnp.float32)
        + from_prev.astype(jnp.float32)
        + from_next.astype(jnp.float32)
        + jnp.concatenate([got_a, got_b], axis=0).astype(jnp.float32)
    )
    return total.astype(jnp.bfloat16)


def partner_swap(block, axis):
    size = lax.axis_size(axis)
    return lax.ppermute(block, axis, [(i, i ^ 1) for i in range(size)])


def even_to_odd(block, axis):
    size = lax.axis_size(axis)
    return lax.ppermute(block, axis, [(i, i + 1) for i in range(0, size - 1, 2)])


def odd_to_even(block, axis):
    size = lax.axis_size(axis)
    return lax.ppermute(block, axis, [(i, i - 1) for i in range(1, size, 2)])


def attn_kernel(sel_ref, q_ref, k0_ref, v0_ref, *refs):
    n_cand = 5
    cand_k = refs[0:2 * n_cand:2]
    cand_v = refs[1:2 * n_cand:2]
    g_ref, srow_ref, scol_ref, attn_ref, dq_ref, self_ref, near_ref, far_ref = refs[2 * n_cand:]
    scale = HEAD_DIM ** (-0.5)

    def pick(cands, slot):
        idx = sel_ref[slot]
        out = cands[0][...]
        for c in range(1, n_cand):
            out = jnp.where(idx == c, cands[c][...], out)
        return out

    ks = [k0_ref[...], pick(cand_k, 0), pick(cand_k, 1)]
    vs = [v0_ref[...], pick(cand_v, 0), pick(cand_v, 1)]
    q = q_ref[...]
    g = g_ref[...]
    nt = (((1,), (1,)), ((), ()))
    tn = (((0,), (0,)), ((), ()))
    scores = [lax.dot_general(q, k, nt, preferred_element_type=jnp.float32) * scale for k in ks]
    visible = srow_ref[...] == scol_ref[...]
    scores[0] = jnp.where(visible, scores[0], NEG_BIG)
    top = jnp.max(scores[0], axis=1, keepdims=True)
    for s in scores[1:]:
        top = jnp.maximum(top, jnp.max(s, axis=1, keepdims=True))
    weights = [jnp.exp(s - top) for s in scores]
    weights[0] = jnp.where(visible, weights[0], 0.0)
    total = weights[0].sum(axis=1, keepdims=True)
    for w in weights[1:]:
        total = total + w.sum(axis=1, keepdims=True)
    inv = 1.0 / total
    probs = [w * inv for w in weights]
    low = [p.astype(jnp.bfloat16) for p in probs]
    acc = jnp.dot(low[0], vs[0], preferred_element_type=jnp.float32)
    for j in (1, 2):
        acc = acc + jnp.dot(low[j], vs[j], preferred_element_type=jnp.float32)
    attn = acc.astype(jnp.bfloat16)
    attn_ref[...] = attn
    gf = g.astype(jnp.float32)
    delta = jnp.sum(attn.astype(jnp.float32) * gf, axis=1, keepdims=True)
    dq = None
    routed = []
    for j in range(3):
        dp = lax.dot_general(g, vs[j], nt, preferred_element_type=jnp.float32)
        ds = (probs[j] * (dp - delta) * scale).astype(jnp.bfloat16)
        part = jnp.dot(ds, ks[j], preferred_element_type=jnp.float32)
        dq = part if dq is None else dq + part
        dk = lax.dot_general(ds, q, tn, preferred_element_type=jnp.float32)
        dv = lax.dot_general(low[j], g, tn, preferred_element_type=jnp.float32)
        if j == 0:
            self_ref[0] = dk
            self_ref[1] = dv
        else:
            routed.append((sel_ref[2 + j], dk.astype(jnp.bfloat16), dv.astype(jnp.bfloat16)))
    (off1, dk1, dv1), (off2, dk2, dv2) = routed
    zero = jnp.zeros_like(dk1)
    for ref, slot, value in ((far_ref, 0, -2), (near_ref, 0, -1), (near_ref, 1, 1), (far_ref, 1, 2)):
        ref[slot, 0] = jnp.where(off1 == value, dk1, jnp.where(off2 == value, dk2, zero))
        ref[slot, 1] = jnp.where(off1 == value, dv1, jnp.where(off2 == value, dv2, zero))
    dq_ref[...] = dq.astype(jnp.bfloat16)


def attention(sel, queries, keys, values, cands, grad_attn, shot_ids):
    rows, columns = queries.shape
    heads = columns // HEAD_DIM
    d = HEAD_DIM
    spec_q = pl.BlockSpec((rows, d), lambda h, s: (0, h))
    spec_ck = pl.BlockSpec((None, rows, d), lambda h, s: (0, 0, h))
    spec_cv = pl.BlockSpec((None, rows, d), lambda h, s: (1, 0, h))
    spec_self = pl.BlockSpec((2, rows, d), lambda h, s: (0, 0, h))
    spec_terms = pl.BlockSpec((2, 2, rows, d), lambda h, s: (0, 0, 0, h))
    cand_specs = []
    cand_args = []
    for c in cands:
        cand_specs += [spec_ck, spec_cv]
        cand_args += [c, c]
    grid_spec = pltpu.PrefetchScalarGridSpec(
        num_scalar_prefetch=1,
        grid=(heads,),
        in_specs=[spec_q, spec_q, spec_q] + cand_specs + [spec_q,
                  pl.BlockSpec((rows, 1), lambda h, s: (0, 0)),
                  pl.BlockSpec((1, rows), lambda h, s: (0, 0))],
        out_specs=[spec_q, spec_q, spec_self, spec_terms, spec_terms],
    )
    out_shape = [
        jax.ShapeDtypeStruct((rows, columns), jnp.bfloat16),
        jax.ShapeDtypeStruct((rows, columns), jnp.bfloat16),
        jax.ShapeDtypeStruct((2, rows, columns), jnp.float32),
        jax.ShapeDtypeStruct((2, 2, rows, columns), jnp.bfloat16),
        jax.ShapeDtypeStruct((2, 2, rows, columns), jnp.bfloat16),
    ]
    kwargs = {}
    if INTERPRET is not None:
        kwargs["interpret"] = INTERPRET
    return pl.pallas_call(
        attn_kernel,
        grid_spec=grid_spec,
        out_shape=out_shape,
        compiler_params=pltpu.CompilerParams(vmem_limit_bytes=48 * 1024 * 1024),
        **kwargs,
    )(sel, queries, keys, values, *cand_args, grad_attn, shot_ids.reshape(rows, 1), shot_ids.reshape(1, rows))


def routed_chunk(queries, keys, values, grad_attn, shot_ids, offs, parity):
    own_kv = jnp.stack([keys, values])
    from_left2 = shifted(own_kv, "seq", 2)
    from_right2 = shifted(own_kv, "seq", -2)
    partner_own = partner_swap(own_kv, "seq")
    relay_to_odd = even_to_odd(from_right2, "seq")
    relay_to_even = odd_to_even(from_left2, "seq")
    partner_off = 1 - 2 * parity
    relay_idx = jnp.where(parity == 1, 2, 3)
    pick = jnp.where(offs == -2, 0, jnp.where(offs == 2, 4, jnp.where(offs == partner_off, 1, relay_idx)))
    sel = jnp.concatenate([pick.astype(jnp.int32), jnp.zeros((1,), jnp.int32), offs])
    cands = (from_left2, partner_own, relay_to_odd, relay_to_even, from_right2)
    attn, grad_q, self_term, near, far = attention(sel, queries, keys, values, cands, grad_attn, shot_ids)
    got_a = even_to_odd(near, "seq")
    got_b = odd_to_even(near, "seq")
    up_plus = (far[1].astype(jnp.float32) + got_b[1].astype(jnp.float32)).astype(jnp.bfloat16)
    up_minus = (far[0].astype(jnp.float32) + got_a[0].astype(jnp.float32)).astype(jnp.bfloat16)
    got_from_left = shifted(up_plus, "seq", 2)
    got_from_right = shifted(up_minus, "seq", -2)
    total = (
        self_term
        + got_a[1].astype(jnp.float32)
        + got_b[0].astype(jnp.float32)
        + got_from_left.astype(jnp.float32)
        + got_from_right.astype(jnp.float32)
    )
    rounded = total.astype(jnp.bfloat16)
    return attn, grad_q, rounded[0], rounded[1]


def on_device(queries, keys, values, out_weight, cotangent, routes, shot_ids):
    seq_index = lax.axis_index("seq")
    parity = seq_index % 2
    columns = queries.shape[1]
    grad_attn = fold_cotangent(cotangent, out_weight)
    offs = (routes[seq_index] - seq_index).astype(jnp.int32)
    bounds = [0, HEAD_DIM, columns] if columns > HEAD_DIM else [0, columns]
    pieces = []
    for lo, hi in zip(bounds[:-1], bounds[1:]):
        pieces.append(routed_chunk(
            queries[:, lo:hi], keys[:, lo:hi], values[:, lo:hi], grad_attn[:, lo:hi],
            shot_ids, offs, parity,
        ))
    attn, grad_q, grad_keys, grad_values = [jnp.concatenate(p, axis=1) for p in zip(*pieces)]
    attn_out = project_out(attn, out_weight)
    return (attn_out, grad_q, grad_keys, grad_values)


def solution(mesh):
    in_specs = (
        P("seq", "head"),
        P("seq", "head"),
        P("seq", "head"),
        P("head", None),
        P("seq", "head"),
        P(),
        P("seq"),
    )
    out_specs = (P("seq", "head"), P("seq", "head"), P("seq", "head"), P("seq", "head"))

    return jax.shard_map(on_device, mesh=mesh, in_specs=in_specs, out_specs=out_specs, check_vma=False)
```

```python
import jax
import jax.numpy as jnp
from jax import lax
from jax.experimental import pallas as pl
from jax.experimental.pallas import tpu as pltpu
from jax.sharding import PartitionSpec as P


HEAD_DIM = 128
NEG_BIG = -1e30
INTERPRET = None


def shifted(block, axis, distance):
    devices = range(lax.axis_size(axis))
    route = [(i - distance, i) for i in devices if i - distance in devices]
    return lax.ppermute(block, axis, route)


def ring_shift(block, axis, distance):
    size = lax.axis_size(axis)
    return lax.ppermute(block, axis, [(i, (i + distance) % size) for i in range(size)])


def head_slice(array, group, width):
    return lax.dynamic_slice_in_dim(array, group * width, width, 1)


def fold_cotangent(cotangent, out_weight):
    groups = lax.axis_size("head")
    me = lax.axis_index("head")
    _, width = cotangent.shape
    from_prev = ring_shift(cotangent, "head", 1)
    from_next = ring_shift(cotangent, "head", -1)
    far = ring_shift(cotangent, "head", 2)
    nt = (((1,), (1,)), ((), ()))
    acc = None
    for piece, group in ((cotangent, me), (from_prev, me - 1), (from_next, me + 1), (far, me + 2)):
        w_cols = head_slice(out_weight, group % groups, width)
        part = lax.dot_general(piece, w_cols, nt, preferred_element_type=jnp.float32)
        acc = part if acc is None else acc + part
    return acc.astype(jnp.bfloat16)


def project_out(attn, out_weight):
    groups = lax.axis_size("head")
    me = lax.axis_index("head")
    _, width = attn.shape

    def part(group):
        w_cols = head_slice(out_weight, group % groups, width)
        return jnp.dot(attn, w_cols, preferred_element_type=jnp.float32).astype(jnp.bfloat16)

    far = part(me + 2)
    near_up = part(me + 1)
    near_down = part(me - 1)
    got_far = ring_shift(far, "head", 2)
    from_prev = ring_shift(near_up, "head", 1)
    from_next = ring_shift(near_down, "head", -1)
    total = (
        jnp.dot(attn, head_slice(out_weight, me, width), preferred_element_type=jnp.float32)
        + from_prev.astype(jnp.float32)
        + from_next.astype(jnp.float32)
        + got_far.astype(jnp.float32)
    )
    return total.astype(jnp.bfloat16)


def partner_swap(block, axis):
    size = lax.axis_size(axis)
    return lax.ppermute(block, axis, [(i, i ^ 1) for i in range(size)])


def even_to_odd(block, axis):
    size = lax.axis_size(axis)
    return lax.ppermute(block, axis, [(i, i + 1) for i in range(0, size - 1, 2)])


def odd_to_even(block, axis):
    size = lax.axis_size(axis)
    return lax.ppermute(block, axis, [(i, i - 1) for i in range(1, size, 2)])


def attn_kernel(sel_ref, q_ref, k0_ref, v0_ref, *refs):
    n_cand = 5
    cand_k = refs[0:2 * n_cand:2]
    cand_v = refs[1:2 * n_cand:2]
    g_ref, srow_ref, scol_ref, attn_ref, dq_ref, self_ref, near_ref, far_ref = refs[2 * n_cand:]
    scale = HEAD_DIM ** (-0.5)

    def pick(cands, slot):
        idx = sel_ref[slot]
        out = cands[0][...]
        for c in range(1, n_cand):
            out = jnp.where(idx == c, cands[c][...], out)
        return out

    ks = [k0_ref[...], pick(cand_k, 0), pick(cand_k, 1)]
    vs = [v0_ref[...], pick(cand_v, 0), pick(cand_v, 1)]
    q = q_ref[...]
    g = g_ref[...]
    nt = (((1,), (1,)), ((), ()))
    tn = (((0,), (0,)), ((), ()))
    scores = [lax.dot_general(q, k, nt, preferred_element_type=jnp.float32) * scale for k in ks]
    visible = srow_ref[...] == scol_ref[...]
    scores[0] = jnp.where(visible, scores[0], NEG_BIG)
    top = jnp.max(scores[0], axis=1, keepdims=True)
    for s in scores[1:]:
        top = jnp.maximum(top, jnp.max(s, axis=1, keepdims=True))
    weights = [jnp.exp(s - top) for s in scores]
    weights[0] = jnp.where(visible, weights[0], 0.0)
    total = weights[0].sum(axis=1, keepdims=True)
    for w in weights[1:]:
        total = total + w.sum(axis=1, keepdims=True)
    inv = 1.0 / total
    probs = [w * inv for w in weights]
    low = [p.astype(jnp.bfloat16) for p in probs]
    acc = jnp.dot(low[0], vs[0], preferred_element_type=jnp.float32)
    for j in (1, 2):
        acc = acc + jnp.dot(low[j], vs[j], preferred_element_type=jnp.float32)
    attn = acc.astype(jnp.bfloat16)
    attn_ref[...] = attn
    gf = g.astype(jnp.float32)
    delta = jnp.sum(attn.astype(jnp.float32) * gf, axis=1, keepdims=True)
    dq = None
    routed = []
    for j in range(3):
        dp = lax.dot_general(g, vs[j], nt, preferred_element_type=jnp.float32)
        ds = (probs[j] * (dp - delta) * scale).astype(jnp.bfloat16)
        part = jnp.dot(ds, ks[j], preferred_element_type=jnp.float32)
        dq = part if dq is None else dq + part
        dk = lax.dot_general(ds, q, tn, preferred_element_type=jnp.float32)
        dv = lax.dot_general(low[j], g, tn, preferred_element_type=jnp.float32)
        if j == 0:
            self_ref[0] = dk
            self_ref[1] = dv
        else:
            routed.append((sel_ref[2 + j], dk.astype(jnp.bfloat16), dv.astype(jnp.bfloat16)))
    (off1, dk1, dv1), (off2, dk2, dv2) = routed
    zero = jnp.zeros_like(dk1)
    for ref, slot, value in ((far_ref, 0, -2), (near_ref, 0, -1), (near_ref, 1, 1), (far_ref, 1, 2)):
        ref[slot, 0] = jnp.where(off1 == value, dk1, jnp.where(off2 == value, dk2, zero))
        ref[slot, 1] = jnp.where(off1 == value, dv1, jnp.where(off2 == value, dv2, zero))
    dq_ref[...] = dq.astype(jnp.bfloat16)


def attention(sel, queries, keys, values, cands, grad_attn, shot_ids):
    rows, columns = queries.shape
    heads = columns // HEAD_DIM
    d = HEAD_DIM
    spec_q = pl.BlockSpec((rows, d), lambda h, s: (0, h))
    spec_ck = pl.BlockSpec((None, rows, d), lambda h, s: (0, 0, h))
    spec_cv = pl.BlockSpec((None, rows, d), lambda h, s: (1, 0, h))
    spec_self = pl.BlockSpec((2, rows, d), lambda h, s: (0, 0, h))
    spec_terms = pl.BlockSpec((2, 2, rows, d), lambda h, s: (0, 0, 0, h))
    cand_specs = []
    cand_args = []
    for c in cands:
        cand_specs += [spec_ck, spec_cv]
        cand_args += [c, c]
    grid_spec = pltpu.PrefetchScalarGridSpec(
        num_scalar_prefetch=1,
        grid=(heads,),
        in_specs=[spec_q, spec_q, spec_q] + cand_specs + [spec_q,
                  pl.BlockSpec((rows, 1), lambda h, s: (0, 0)),
                  pl.BlockSpec((1, rows), lambda h, s: (0, 0))],
        out_specs=[spec_q, spec_q, spec_self, spec_terms, spec_terms],
    )
    out_shape = [
        jax.ShapeDtypeStruct((rows, columns), jnp.bfloat16),
        jax.ShapeDtypeStruct((rows, columns), jnp.bfloat16),
        jax.ShapeDtypeStruct((2, rows, columns), jnp.float32),
        jax.ShapeDtypeStruct((2, 2, rows, columns), jnp.bfloat16),
        jax.ShapeDtypeStruct((2, 2, rows, columns), jnp.bfloat16),
    ]
    kwargs = {}
    if INTERPRET is not None:
        kwargs["interpret"] = INTERPRET
    return pl.pallas_call(
        attn_kernel,
        grid_spec=grid_spec,
        out_shape=out_shape,
        compiler_params=pltpu.CompilerParams(vmem_limit_bytes=48 * 1024 * 1024),
        **kwargs,
    )(sel, queries, keys, values, *cand_args, grad_attn, shot_ids.reshape(rows, 1), shot_ids.reshape(1, rows))


def on_device(queries, keys, values, out_weight, cotangent, routes, shot_ids):
    seq_index = lax.axis_index("seq")
    parity = seq_index % 2
    grad_attn = fold_cotangent(cotangent, out_weight)
    own_kv = jnp.stack([keys, values])
    from_left2 = shifted(own_kv, "seq", 2)
    from_right2 = shifted(own_kv, "seq", -2)
    partner_own = partner_swap(own_kv, "seq")
    relay_to_odd = even_to_odd(from_right2, "seq")
    relay_to_even = odd_to_even(from_left2, "seq")
    partner_off = 1 - 2 * parity
    offs = (routes[seq_index] - seq_index).astype(jnp.int32)
    relay_idx = jnp.where(parity == 1, 2, 3)
    pick = jnp.where(offs == -2, 0, jnp.where(offs == 2, 4, jnp.where(offs == partner_off, 1, relay_idx)))
    sel = jnp.concatenate([pick.astype(jnp.int32), jnp.zeros((1,), jnp.int32), offs])
    cands = (from_left2, partner_own, relay_to_odd, relay_to_even, from_right2)
    attn, grad_q, self_term, near, far = attention(sel, queries, keys, values, cands, grad_attn, shot_ids)
    attn_out = project_out(attn, out_weight)
    got_a = even_to_odd(near, "seq")
    got_b = odd_to_even(near, "seq")
    up_plus = (far[1].astype(jnp.float32) + got_b[1].astype(jnp.float32)).astype(jnp.bfloat16)
    up_minus = (far[0].astype(jnp.float32) + got_a[0].astype(jnp.float32)).astype(jnp.bfloat16)
    got_from_left = shifted(up_plus, "seq", 2)
    got_from_right = shifted(up_minus, "seq", -2)
    total = (
        self_term
        + got_a[1].astype(jnp.float32)
        + got_b[0].astype(jnp.float32)
        + got_from_left.astype(jnp.float32)
        + got_from_right.astype(jnp.float32)
    )
    rounded = total.astype(jnp.bfloat16)
    return (attn_out, grad_q, rounded[0], rounded[1])


def solution(mesh):
    in_specs = (
        P("seq", "head"),
        P("seq", "head"),
        P("seq", "head"),
        P("head", None),
        P("seq", "head"),
        P(),
        P("seq"),
    )
    out_specs = (P("seq", "head"), P("seq", "head"), P("seq", "head"), P("seq", "head"))

    return jax.shard_map(on_device, mesh=mesh, in_specs=in_specs, out_specs=out_specs, check_vma=False)
```

```python
import jax
import jax.numpy as jnp
from jax import lax
from jax.experimental import pallas as pl
from jax.experimental.pallas import tpu as pltpu
from jax.sharding import PartitionSpec as P


HEAD_DIM = 128
NEG_BIG = -1e30
INTERPRET = None


def shifted(block, axis, distance):
    devices = range(lax.axis_size(axis))
    route = [(i - distance, i) for i in devices if i - distance in devices]
    return lax.ppermute(block, axis, route)


def ring_shift(block, axis, distance):
    size = lax.axis_size(axis)
    return lax.ppermute(block, axis, [(i, (i + distance) % size) for i in range(size)])


def head_slice(array, group, width):
    return lax.dynamic_slice_in_dim(array, group * width, width, 1)


def fold_cotangent(cotangent, out_weight):
    groups = lax.axis_size("head")
    me = lax.axis_index("head")
    _, width = cotangent.shape
    from_prev = ring_shift(cotangent, "head", 1)
    from_next = ring_shift(cotangent, "head", -1)
    far = ring_shift(cotangent, "head", 2)
    nt = (((1,), (1,)), ((), ()))
    acc = None
    for piece, group in ((cotangent, me), (from_prev, me - 1), (from_next, me + 1), (far, me + 2)):
        w_cols = head_slice(out_weight, group % groups, width)
        part = lax.dot_general(piece, w_cols, nt, preferred_element_type=jnp.float32)
        acc = part if acc is None else acc + part
    return acc.astype(jnp.bfloat16)


def project_out(attn, out_weight):
    groups = lax.axis_size("head")
    me = lax.axis_index("head")
    _, width = attn.shape

    def part(group):
        w_cols = head_slice(out_weight, group % groups, width)
        return jnp.dot(attn, w_cols, preferred_element_type=jnp.float32).astype(jnp.bfloat16)

    far = part(me + 2)
    near_up = part(me + 1)
    near_down = part(me - 1)
    got_far = ring_shift(far, "head", 2)
    from_prev = ring_shift(near_up, "head", 1)
    from_next = ring_shift(near_down, "head", -1)
    total = (
        jnp.dot(attn, head_slice(out_weight, me, width), preferred_element_type=jnp.float32)
        + from_prev.astype(jnp.float32)
        + from_next.astype(jnp.float32)
        + got_far.astype(jnp.float32)
    )
    return total.astype(jnp.bfloat16)


def partner_swap(block, axis):
    size = lax.axis_size(axis)
    return lax.ppermute(block, axis, [(i, i ^ 1) for i in range(size)])


def cross_chip(block, axis):
    size = lax.axis_size(axis)
    pairs = [(i, i - 1) for i in range(2, size, 2)] + [(i, i + 1) for i in range(1, size - 1, 2)]
    return lax.ppermute(block, axis, pairs)


def attn_kernel(sel_ref, q_ref, k0_ref, v0_ref, *refs):
    n_cand = 4
    cand_k = refs[0:2 * n_cand:2]
    cand_v = refs[1:2 * n_cand:2]
    g_ref, srow_ref, scol_ref, attn_ref, dq_ref, self_ref, near_ref, far_ref = refs[2 * n_cand:]
    scale = HEAD_DIM ** (-0.5)

    def pick(cands, slot):
        idx = sel_ref[slot]
        out = cands[0][...]
        for c in range(1, n_cand):
            out = jnp.where(idx == c, cands[c][...], out)
        return out

    ks = [k0_ref[...], pick(cand_k, 0), pick(cand_k, 1)]
    vs = [v0_ref[...], pick(cand_v, 0), pick(cand_v, 1)]
    q = q_ref[...]
    g = g_ref[...]
    nt = (((1,), (1,)), ((), ()))
    tn = (((0,), (0,)), ((), ()))
    scores = [lax.dot_general(q, k, nt, preferred_element_type=jnp.float32) * scale for k in ks]
    visible = srow_ref[...] == scol_ref[...]
    scores[0] = jnp.where(visible, scores[0], NEG_BIG)
    top = jnp.max(scores[0], axis=1, keepdims=True)
    for s in scores[1:]:
        top = jnp.maximum(top, jnp.max(s, axis=1, keepdims=True))
    weights = [jnp.exp(s - top) for s in scores]
    weights[0] = jnp.where(visible, weights[0], 0.0)
    total = weights[0].sum(axis=1, keepdims=True)
    for w in weights[1:]:
        total = total + w.sum(axis=1, keepdims=True)
    inv = 1.0 / total
    probs = [w * inv for w in weights]
    low = [p.astype(jnp.bfloat16) for p in probs]
    acc = jnp.dot(low[0], vs[0], preferred_element_type=jnp.float32)
    for j in (1, 2):
        acc = acc + jnp.dot(low[j], vs[j], preferred_element_type=jnp.float32)
    attn = acc.astype(jnp.bfloat16)
    attn_ref[...] = attn
    gf = g.astype(jnp.float32)
    delta = jnp.sum(attn.astype(jnp.float32) * gf, axis=1, keepdims=True)
    dq = None
    routed = []
    for j in range(3):
        dp = lax.dot_general(g, vs[j], nt, preferred_element_type=jnp.float32)
        ds = (probs[j] * (dp - delta) * scale).astype(jnp.bfloat16)
        part = jnp.dot(ds, ks[j], preferred_element_type=jnp.float32)
        dq = part if dq is None else dq + part
        dk = lax.dot_general(ds, q, tn, preferred_element_type=jnp.float32)
        dv = lax.dot_general(low[j], g, tn, preferred_element_type=jnp.float32)
        if j == 0:
            self_ref[0] = dk
            self_ref[1] = dv
        else:
            routed.append((sel_ref[2 + j], dk.astype(jnp.bfloat16), dv.astype(jnp.bfloat16)))
    (off1, dk1, dv1), (off2, dk2, dv2) = routed
    zero = jnp.zeros_like(dk1)
    partner_off = 1 - 2 * sel_ref[5]
    for ref, slot, value in ((far_ref, 0, -2), (near_ref, 0, partner_off), (near_ref, 1, -partner_off),
                             (far_ref, 1, 2)):
        ref[slot, 0] = jnp.where(off1 == value, dk1, jnp.where(off2 == value, dk2, zero))
        ref[slot, 1] = jnp.where(off1 == value, dv1, jnp.where(off2 == value, dv2, zero))
    dq_ref[...] = dq.astype(jnp.bfloat16)


def attention(sel, queries, keys, values, cands, grad_attn, shot_ids):
    rows, columns = queries.shape
    heads = columns // HEAD_DIM
    d = HEAD_DIM
    spec_q = pl.BlockSpec((rows, d), lambda h, s: (0, h))
    spec_ck = pl.BlockSpec((None, rows, d), lambda h, s: (0, 0, h))
    spec_cv = pl.BlockSpec((None, rows, d), lambda h, s: (1, 0, h))
    spec_self = pl.BlockSpec((2, rows, d), lambda h, s: (0, 0, h))
    spec_terms = pl.BlockSpec((2, 2, rows, d), lambda h, s: (0, 0, 0, h))
    cand_specs = []
    cand_args = []
    for c in cands:
        cand_specs += [spec_ck, spec_cv]
        cand_args += [c, c]
    grid_spec = pltpu.PrefetchScalarGridSpec(
        num_scalar_prefetch=1,
        grid=(heads,),
        in_specs=[spec_q, spec_q, spec_q] + cand_specs + [spec_q,
                  pl.BlockSpec((rows, 1), lambda h, s: (0, 0)),
                  pl.BlockSpec((1, rows), lambda h, s: (0, 0))],
        out_specs=[spec_q, spec_q, spec_self, spec_terms, spec_terms],
    )
    out_shape = [
        jax.ShapeDtypeStruct((rows, columns), jnp.bfloat16),
        jax.ShapeDtypeStruct((rows, columns), jnp.bfloat16),
        jax.ShapeDtypeStruct((2, rows, columns), jnp.float32),
        jax.ShapeDtypeStruct((2, 2, rows, columns), jnp.bfloat16),
        jax.ShapeDtypeStruct((2, 2, rows, columns), jnp.bfloat16),
    ]
    kwargs = {}
    if INTERPRET is not None:
        kwargs["interpret"] = INTERPRET
    return pl.pallas_call(
        attn_kernel,
        grid_spec=grid_spec,
        out_shape=out_shape,
        compiler_params=pltpu.CompilerParams(vmem_limit_bytes=48 * 1024 * 1024),
        **kwargs,
    )(sel, queries, keys, values, *cand_args, grad_attn, shot_ids.reshape(rows, 1), shot_ids.reshape(1, rows))


def on_device(queries, keys, values, out_weight, cotangent, routes, shot_ids):
    seq_index = lax.axis_index("seq")
    parity = seq_index % 2
    grad_attn = fold_cotangent(cotangent, out_weight)
    own_kv = jnp.stack([keys, values])
    from_left2 = shifted(own_kv, "seq", 2)
    from_right2 = shifted(own_kv, "seq", -2)
    partner_own = partner_swap(own_kv, "seq")
    from_cross = cross_chip(own_kv, "seq")
    partner_off = 1 - 2 * parity
    offs = (routes[seq_index] - seq_index).astype(jnp.int32)
    pick = jnp.where(offs == -2, 0, jnp.where(offs == 2, 3, jnp.where(offs == partner_off, 1, 2)))
    sel = jnp.concatenate([pick.astype(jnp.int32), jnp.zeros((1,), jnp.int32), offs, parity[None]])
    sel = sel.astype(jnp.int32)
    cands = (from_left2, partner_own, from_cross, from_right2)
    attn, grad_q, self_term, near, far = attention(sel, queries, keys, values, cands, grad_attn, shot_ids)
    attn_out = project_out(attn, out_weight)
    back_partner = partner_swap(near[0], "seq")
    back_cross = cross_chip(near[1], "seq")
    got_from_left = shifted(far[1], "seq", 2)
    got_from_right = shifted(far[0], "seq", -2)
    total = (
        self_term
        + back_partner.astype(jnp.float32)
        + back_cross.astype(jnp.float32)
        + got_from_left.astype(jnp.float32)
        + got_from_right.astype(jnp.float32)
    )
    rounded = total.astype(jnp.bfloat16)
    return (attn_out, grad_q, rounded[0], rounded[1])


def solution(mesh):
    in_specs = (
        P("seq", "head"),
        P("seq", "head"),
        P("seq", "head"),
        P("head", None),
        P("seq", "head"),
        P(),
        P("seq"),
    )
    out_specs = (P("seq", "head"), P("seq", "head"), P("seq", "head"), P("seq", "head"))

    return jax.shard_map(on_device, mesh=mesh, in_specs=in_specs, out_specs=out_specs, check_vma=False)
```

```python
import jax
import jax.numpy as jnp
from jax import lax
from jax.experimental import pallas as pl
from jax.experimental.pallas import tpu as pltpu
from jax.sharding import PartitionSpec as P


HEAD_DIM = 128
NEG_BIG = -1e30
INTERPRET = None


def shifted(block, axis, distance):
    devices = range(lax.axis_size(axis))
    route = [(i - distance, i) for i in devices if i - distance in devices]
    return lax.ppermute(block, axis, route)


def ring_shift(block, axis, distance):
    size = lax.axis_size(axis)
    return lax.ppermute(block, axis, [(i, (i + distance) % size) for i in range(size)])


def head_slice(array, group, width):
    return lax.dynamic_slice_in_dim(array, group * width, width, 1)


def fold_cotangent(cotangent, out_weight):
    groups = lax.axis_size("head")
    me = lax.axis_index("head")
    _, width = cotangent.shape
    from_prev = ring_shift(cotangent, "head", 1)
    from_next = ring_shift(cotangent, "head", -1)
    far = ring_shift(cotangent, "head", 2)
    nt = (((1,), (1,)), ((), ()))
    acc = None
    for piece, group in ((cotangent, me), (from_prev, me - 1), (from_next, me + 1), (far, me + 2)):
        w_cols = head_slice(out_weight, group % groups, width)
        part = lax.dot_general(piece, w_cols, nt, preferred_element_type=jnp.float32)
        acc = part if acc is None else acc + part
    return acc.astype(jnp.bfloat16)


def project_out(attn, out_weight):
    groups = lax.axis_size("head")
    me = lax.axis_index("head")
    _, width = attn.shape

    def part(group):
        w_cols = head_slice(out_weight, group % groups, width)
        return jnp.dot(attn, w_cols, preferred_element_type=jnp.float32).astype(jnp.bfloat16)

    far = part(me + 2)
    near_up = part(me + 1)
    near_down = part(me - 1)
    got_far = ring_shift(far, "head", 2)
    from_prev = ring_shift(near_up, "head", 1)
    from_next = ring_shift(near_down, "head", -1)
    total = (
        jnp.dot(attn, head_slice(out_weight, me, width), preferred_element_type=jnp.float32)
        + from_prev.astype(jnp.float32)
        + from_next.astype(jnp.float32)
        + got_far.astype(jnp.float32)
    )
    return total.astype(jnp.bfloat16)


def partner_swap(block, axis):
    size = lax.axis_size(axis)
    return lax.ppermute(block, axis, [(i, i ^ 1) for i in range(size)])


def even_to_odd(block, axis):
    size = lax.axis_size(axis)
    return lax.ppermute(block, axis, [(i, i + 1) for i in range(0, size - 1, 2)])


def odd_to_even(block, axis):
    size = lax.axis_size(axis)
    return lax.ppermute(block, axis, [(i, i - 1) for i in range(1, size, 2)])


def attn_kernel(sel_ref, q_ref, k0_ref, v0_ref, *refs):
    n_cand = 5
    cand_k = refs[0:2 * n_cand:2]
    cand_v = refs[1:2 * n_cand:2]
    g_ref, srow_ref, scol_ref, attn_ref, dq_ref, self_ref, near_ref, far_ref = refs[2 * n_cand:]
    scale = HEAD_DIM ** (-0.5)

    def pick(cands, slot):
        idx = sel_ref[slot]
        out = cands[0][...]
        for c in range(1, n_cand):
            out = jnp.where(idx == c, cands[c][...], out)
        return out

    ks = [k0_ref[...], pick(cand_k, 0), pick(cand_k, 1)]
    vs = [v0_ref[...], pick(cand_v, 0), pick(cand_v, 1)]
    q = q_ref[...]
    g = g_ref[...]
    nt = (((1,), (1,)), ((), ()))
    tn = (((0,), (0,)), ((), ()))
    scores = [lax.dot_general(q, k, nt, preferred_element_type=jnp.float32) * scale for k in ks]
    visible = srow_ref[...] == scol_ref[...]
    scores[0] = jnp.where(visible, scores[0], NEG_BIG)
    top = jnp.max(scores[0], axis=1, keepdims=True)
    for s in scores[1:]:
        top = jnp.maximum(top, jnp.max(s, axis=1, keepdims=True))
    weights = [jnp.exp(s - top) for s in scores]
    weights[0] = jnp.where(visible, weights[0], 0.0)
    total = weights[0].sum(axis=1, keepdims=True)
    for w in weights[1:]:
        total = total + w.sum(axis=1, keepdims=True)
    inv = 1.0 / total
    probs = [w * inv for w in weights]
    low = [p.astype(jnp.bfloat16) for p in probs]
    acc = jnp.dot(low[0], vs[0], preferred_element_type=jnp.float32)
    for j in (1, 2):
        acc = acc + jnp.dot(low[j], vs[j], preferred_element_type=jnp.float32)
    attn = acc.astype(jnp.bfloat16)
    attn_ref[...] = attn
    gf = g.astype(jnp.float32)
    delta = jnp.sum(attn.astype(jnp.float32) * gf, axis=1, keepdims=True)
    dq = None
    routed = []
    for j in range(3):
        dp = lax.dot_general(g, vs[j], nt, preferred_element_type=jnp.float32)
        ds = (probs[j] * (dp - delta) * scale).astype(jnp.bfloat16)
        part = jnp.dot(ds, ks[j], preferred_element_type=jnp.float32)
        dq = part if dq is None else dq + part
        dk = lax.dot_general(ds, q, tn, preferred_element_type=jnp.float32)
        dv = lax.dot_general(low[j], g, tn, preferred_element_type=jnp.float32)
        if j == 0:
            self_ref[0] = dk
            self_ref[1] = dv
        else:
            routed.append((sel_ref[2 + j], dk.astype(jnp.bfloat16), dv.astype(jnp.bfloat16)))
    (off1, dk1, dv1), (off2, dk2, dv2) = routed
    zero = jnp.zeros_like(dk1)
    for ref, slot, value in ((far_ref, 0, -2), (near_ref, 0, -1), (near_ref, 1, 1), (far_ref, 1, 2)):
        ref[slot, 0] = jnp.where(off1 == value, dk1, jnp.where(off2 == value, dk2, zero))
        ref[slot, 1] = jnp.where(off1 == value, dv1, jnp.where(off2 == value, dv2, zero))
    dq_ref[...] = dq.astype(jnp.bfloat16)


def attention(sel, queries, keys, values, cands, grad_attn, shot_ids):
    rows, columns = queries.shape
    heads = columns // HEAD_DIM
    d = HEAD_DIM
    spec_q = pl.BlockSpec((rows, d), lambda h, s: (0, h))
    spec_ck = pl.BlockSpec((None, rows, d), lambda h, s: (0, 0, h))
    spec_cv = pl.BlockSpec((None, rows, d), lambda h, s: (1, 0, h))
    spec_self = pl.BlockSpec((2, rows, d), lambda h, s: (0, 0, h))
    spec_terms = pl.BlockSpec((2, 2, rows, d), lambda h, s: (0, 0, 0, h))
    cand_specs = []
    cand_args = []
    for c in cands:
        cand_specs += [spec_ck, spec_cv]
        cand_args += [c, c]
    grid_spec = pltpu.PrefetchScalarGridSpec(
        num_scalar_prefetch=1,
        grid=(heads,),
        in_specs=[spec_q, spec_q, spec_q] + cand_specs + [spec_q,
                  pl.BlockSpec((rows, 1), lambda h, s: (0, 0)),
                  pl.BlockSpec((1, rows), lambda h, s: (0, 0))],
        out_specs=[spec_q, spec_q, spec_self, spec_terms, spec_terms],
    )
    out_shape = [
        jax.ShapeDtypeStruct((rows, columns), jnp.bfloat16),
        jax.ShapeDtypeStruct((rows, columns), jnp.bfloat16),
        jax.ShapeDtypeStruct((2, rows, columns), jnp.float32),
        jax.ShapeDtypeStruct((2, 2, rows, columns), jnp.bfloat16),
        jax.ShapeDtypeStruct((2, 2, rows, columns), jnp.bfloat16),
    ]
    kwargs = {}
    if INTERPRET is not None:
        kwargs["interpret"] = INTERPRET
    return pl.pallas_call(
        attn_kernel,
        grid_spec=grid_spec,
        out_shape=out_shape,
        compiler_params=pltpu.CompilerParams(vmem_limit_bytes=48 * 1024 * 1024),
        **kwargs,
    )(sel, queries, keys, values, *cand_args, grad_attn, shot_ids.reshape(rows, 1), shot_ids.reshape(1, rows))


def on_device(queries, keys, values, out_weight, cotangent, routes, shot_ids):
    seq_index = lax.axis_index("seq")
    parity = seq_index % 2
    grad_attn = fold_cotangent(cotangent, out_weight)
    own_kv = jnp.stack([keys, values])
    from_left2 = shifted(own_kv, "seq", 2)
    from_right2 = shifted(own_kv, "seq", -2)
    partner_own = partner_swap(own_kv, "seq")
    relay_to_odd = even_to_odd(from_right2, "seq")
    relay_to_even = odd_to_even(from_left2, "seq")
    partner_off = 1 - 2 * parity
    offs = (routes[seq_index] - seq_index).astype(jnp.int32)
    relay_idx = jnp.where(parity == 1, 2, 3)
    pick = jnp.where(offs == -2, 0, jnp.where(offs == 2, 4, jnp.where(offs == partner_off, 1, relay_idx)))
    sel = jnp.concatenate([pick.astype(jnp.int32), jnp.zeros((1,), jnp.int32), offs])
    cands = (from_left2, partner_own, relay_to_odd, relay_to_even, from_right2)
    attn, grad_q, self_term, near, far = attention(sel, queries, keys, values, cands, grad_attn, shot_ids)
    attn_out = project_out(attn, out_weight)
    got_a = even_to_odd(near, "seq")
    got_b = odd_to_even(near, "seq")
    up_plus = (far[1].astype(jnp.float32) + got_b[1].astype(jnp.float32)).astype(jnp.bfloat16)
    up_minus = (far[0].astype(jnp.float32) + got_a[0].astype(jnp.float32)).astype(jnp.bfloat16)
    got_from_left = shifted(up_plus, "seq", 2)
    got_from_right = shifted(up_minus, "seq", -2)

    def summed(part):
        total = (
            self_term[part]
            + got_a[1, part].astype(jnp.float32)
            + got_b[0, part].astype(jnp.float32)
            + got_from_left[part].astype(jnp.float32)
            + got_from_right[part].astype(jnp.float32)
        )
        return total.astype(jnp.bfloat16)

    return (attn_out, grad_q, summed(0), summed(1))


def solution(mesh):
    in_specs = (
        P("seq", "head"),
        P("seq", "head"),
        P("seq", "head"),
        P("head", None),
        P("seq", "head"),
        P(),
        P("seq"),
    )
    out_specs = (P("seq", "head"), P("seq", "head"), P("seq", "head"), P("seq", "head"))

    return jax.shard_map(on_device, mesh=mesh, in_specs=in_specs, out_specs=out_specs, check_vma=False)
```

```python
import jax
import jax.numpy as jnp
from jax import lax
from jax.experimental import pallas as pl
from jax.experimental.pallas import tpu as pltpu
from jax.sharding import PartitionSpec as P


HEAD_DIM = 128
NEG_BIG = -1e30
INTERPRET = None


def shifted(block, axis, distance):
    devices = range(lax.axis_size(axis))
    route = [(i - distance, i) for i in devices if i - distance in devices]
    return lax.ppermute(block, axis, route)


def ring_shift(block, axis, distance):
    size = lax.axis_size(axis)
    return lax.ppermute(block, axis, [(i, (i + distance) % size) for i in range(size)])


def head_slice(array, group, width):
    return lax.dynamic_slice_in_dim(array, group * width, width, 1)


def fold_cotangent(cotangent, out_weight):
    groups = lax.axis_size("head")
    me = lax.axis_index("head")
    _, width = cotangent.shape
    from_prev = ring_shift(cotangent, "head", 1)
    from_next = ring_shift(cotangent, "head", -1)
    far = ring_shift(cotangent, "head", 2)
    nt = (((1,), (1,)), ((), ()))
    acc = None
    for piece, group in ((cotangent, me), (from_prev, me - 1), (from_next, me + 1), (far, me + 2)):
        w_cols = head_slice(out_weight, group % groups, width)
        part = lax.dot_general(piece, w_cols, nt, preferred_element_type=jnp.float32)
        acc = part if acc is None else acc + part
    return acc.astype(jnp.bfloat16)


def project_out(attn, out_weight):
    groups = lax.axis_size("head")
    me = lax.axis_index("head")
    _, width = attn.shape

    def part(group):
        w_cols = head_slice(out_weight, group % groups, width)
        return jnp.dot(attn, w_cols, preferred_element_type=jnp.float32).astype(jnp.bfloat16)

    far = part(me + 2)
    near_up = part(me + 1)
    near_down = part(me - 1)
    got_far = ring_shift(far, "head", 2)
    from_prev = ring_shift(near_up, "head", 1)
    from_next = ring_shift(near_down, "head", -1)
    total = (
        jnp.dot(attn, head_slice(out_weight, me, width), preferred_element_type=jnp.float32)
        + from_prev.astype(jnp.float32)
        + from_next.astype(jnp.float32)
        + got_far.astype(jnp.float32)
    )
    return total.astype(jnp.bfloat16)


def partner_swap(block, axis):
    size = lax.axis_size(axis)
    return lax.ppermute(block, axis, [(i, i ^ 1) for i in range(size)])


def even_to_odd(block, axis):
    size = lax.axis_size(axis)
    return lax.ppermute(block, axis, [(i, i + 1) for i in range(0, size - 1, 2)])


def odd_to_even(block, axis):
    size = lax.axis_size(axis)
    return lax.ppermute(block, axis, [(i, i - 1) for i in range(1, size, 2)])


def attn_kernel(sel_ref, q_ref, k0_ref, v0_ref, *refs):
    n_cand = 5
    cand_k = refs[0:2 * n_cand:2]
    cand_v = refs[1:2 * n_cand:2]
    g_ref, srow_ref, scol_ref, attn_ref, dq_ref, self_ref, near_ref, far_ref = refs[2 * n_cand:]
    scale = HEAD_DIM ** (-0.5)

    def pick(cands, slot):
        idx = sel_ref[slot]
        out = cands[0][...]
        for c in range(1, n_cand):
            out = jnp.where(idx == c, cands[c][...], out)
        return out

    ks = [k0_ref[...], pick(cand_k, 0), pick(cand_k, 1)]
    vs = [v0_ref[...], pick(cand_v, 0), pick(cand_v, 1)]
    q = q_ref[...]
    g = g_ref[...]
    nt = (((1,), (1,)), ((), ()))
    tn = (((0,), (0,)), ((), ()))
    scores = [lax.dot_general(q, k, nt, preferred_element_type=jnp.float32) * scale for k in ks]
    visible = srow_ref[...] == scol_ref[...]
    scores[0] = jnp.where(visible, scores[0], NEG_BIG)
    top = jnp.max(scores[0], axis=1, keepdims=True)
    for s in scores[1:]:
        top = jnp.maximum(top, jnp.max(s, axis=1, keepdims=True))
    weights = [jnp.exp(s - top) for s in scores]
    weights[0] = jnp.where(visible, weights[0], 0.0)
    total = weights[0].sum(axis=1, keepdims=True)
    for w in weights[1:]:
        total = total + w.sum(axis=1, keepdims=True)
    inv = 1.0 / total
    probs = [w * inv for w in weights]
    low = [p.astype(jnp.bfloat16) for p in probs]
    acc = jnp.dot(low[0], vs[0], preferred_element_type=jnp.float32)
    for j in (1, 2):
        acc = acc + jnp.dot(low[j], vs[j], preferred_element_type=jnp.float32)
    attn = acc.astype(jnp.bfloat16)
    attn_ref[...] = attn
    gf = g.astype(jnp.float32)
    delta = jnp.sum(attn.astype(jnp.float32) * gf, axis=1, keepdims=True)
    dq = None
    routed = []
    for j in range(3):
        dp = lax.dot_general(g, vs[j], nt, preferred_element_type=jnp.float32)
        ds = (probs[j] * (dp - delta) * scale).astype(jnp.bfloat16)
        part = jnp.dot(ds, ks[j], preferred_element_type=jnp.float32)
        dq = part if dq is None else dq + part
        dk = lax.dot_general(ds, q, tn, preferred_element_type=jnp.float32)
        dv = lax.dot_general(low[j], g, tn, preferred_element_type=jnp.float32)
        if j == 0:
            self_ref[0] = dk
            self_ref[1] = dv
        else:
            routed.append((sel_ref[2 + j], dk.astype(jnp.bfloat16), dv.astype(jnp.bfloat16)))
    (off1, dk1, dv1), (off2, dk2, dv2) = routed
    zero = jnp.zeros_like(dk1)
    for ref, slot, value in ((far_ref, 0, -2), (near_ref, 0, -1), (near_ref, 1, 1), (far_ref, 1, 2)):
        ref[slot, 0] = jnp.where(off1 == value, dk1, jnp.where(off2 == value, dk2, zero))
        ref[slot, 1] = jnp.where(off1 == value, dv1, jnp.where(off2 == value, dv2, zero))
    dq_ref[...] = dq.astype(jnp.bfloat16)


def attention(sel, queries, keys, values, cands, grad_attn, shot_ids):
    rows, columns = queries.shape
    heads = columns // HEAD_DIM
    d = HEAD_DIM
    spec_q = pl.BlockSpec((rows, d), lambda h, s: (0, h))
    spec_ck = pl.BlockSpec((None, rows, d), lambda h, s: (0, 0, h))
    spec_cv = pl.BlockSpec((None, rows, d), lambda h, s: (1, 0, h))
    spec_self = pl.BlockSpec((2, rows, d), lambda h, s: (0, 0, h))
    spec_terms = pl.BlockSpec((2, 2, rows, d), lambda h, s: (0, 0, 0, h))
    cand_specs = []
    cand_args = []
    for c in cands:
        cand_specs += [spec_ck, spec_cv]
        cand_args += [c, c]
    grid_spec = pltpu.PrefetchScalarGridSpec(
        num_scalar_prefetch=1,
        grid=(heads,),
        in_specs=[spec_q, spec_q, spec_q] + cand_specs + [spec_q,
                  pl.BlockSpec((rows, 1), lambda h, s: (0, 0)),
                  pl.BlockSpec((1, rows), lambda h, s: (0, 0))],
        out_specs=[spec_q, spec_q, spec_self, spec_terms, spec_terms],
    )
    out_shape = [
        jax.ShapeDtypeStruct((rows, columns), jnp.bfloat16),
        jax.ShapeDtypeStruct((rows, columns), jnp.bfloat16),
        jax.ShapeDtypeStruct((2, rows, columns), jnp.float32),
        jax.ShapeDtypeStruct((2, 2, rows, columns), jnp.bfloat16),
        jax.ShapeDtypeStruct((2, 2, rows, columns), jnp.bfloat16),
    ]
    kwargs = {}
    if INTERPRET is not None:
        kwargs["interpret"] = INTERPRET
    return pl.pallas_call(
        attn_kernel,
        grid_spec=grid_spec,
        out_shape=out_shape,
        compiler_params=pltpu.CompilerParams(vmem_limit_bytes=48 * 1024 * 1024),
        **kwargs,
    )(sel, queries, keys, values, *cand_args, grad_attn, shot_ids.reshape(rows, 1), shot_ids.reshape(1, rows))


def on_device(queries, keys, values, out_weight, cotangent, routes, shot_ids):
    seq_index = lax.axis_index("seq")
    parity = seq_index % 2
    grad_attn = fold_cotangent(cotangent, out_weight)
    own_kv = jnp.stack([keys, values])
    from_left2 = shifted(own_kv, "seq", 2)
    from_right2 = shifted(own_kv, "seq", -2)
    partner_own = partner_swap(own_kv, "seq")
    relay_to_odd = even_to_odd(from_right2, "seq")
    relay_to_even = odd_to_even(from_left2, "seq")
    partner_off = 1 - 2 * parity
    offs = (routes[seq_index] - seq_index).astype(jnp.int32)
    relay_idx = jnp.where(parity == 1, 2, 3)
    pick = jnp.where(offs == -2, 0, jnp.where(offs == 2, 4, jnp.where(offs == partner_off, 1, relay_idx)))
    sel = jnp.concatenate([pick.astype(jnp.int32), jnp.zeros((1,), jnp.int32), offs])
    cands = (from_left2, partner_own, relay_to_odd, relay_to_even, from_right2)
    attn, grad_q, self_term, near, far = attention(sel, queries, keys, values, cands, grad_attn, shot_ids)
    attn_out = project_out(attn, out_weight)
    got = partner_swap(near, "seq").astype(jnp.float32)
    odd = parity == 1
    up_plus = (far[1].astype(jnp.float32) + jnp.where(odd, 0.0, got[1])).astype(jnp.bfloat16)
    up_minus = (far[0].astype(jnp.float32) + jnp.where(odd, got[0], 0.0)).astype(jnp.bfloat16)
    got_from_left = shifted(up_plus, "seq", 2)
    got_from_right = shifted(up_minus, "seq", -2)
    total = (
        self_term
        + jnp.where(odd, got[1], got[0])
        + got_from_left.astype(jnp.float32)
        + got_from_right.astype(jnp.float32)
    )
    rounded = total.astype(jnp.bfloat16)
    return (attn_out, grad_q, rounded[0], rounded[1])


def solution(mesh):
    in_specs = (
        P("seq", "head"),
        P("seq", "head"),
        P("seq", "head"),
        P("head", None),
        P("seq", "head"),
        P(),
        P("seq"),
    )
    out_specs = (P("seq", "head"), P("seq", "head"), P("seq", "head"), P("seq", "head"))

    return jax.shard_map(on_device, mesh=mesh, in_specs=in_specs, out_specs=out_specs, check_vma=False)
```

```python
import jax
import jax.numpy as jnp
from jax import lax
from jax.experimental import pallas as pl
from jax.experimental.pallas import tpu as pltpu
from jax.sharding import PartitionSpec as P


HEAD_DIM = 128
NEG_BIG = -1e30
INTERPRET = None


def shifted(block, axis, distance):
    devices = range(lax.axis_size(axis))
    route = [(i - distance, i) for i in devices if i - distance in devices]
    return lax.ppermute(block, axis, route)


def ring_shift(block, axis, distance):
    size = lax.axis_size(axis)
    return lax.ppermute(block, axis, [(i, (i + distance) % size) for i in range(size)])


def head_slice(array, group, width):
    return lax.dynamic_slice_in_dim(array, group * width, width, 1)


def fold_cotangent(cotangent, out_weight):
    groups = lax.axis_size("head")
    me = lax.axis_index("head")
    _, width = cotangent.shape
    from_prev = ring_shift(cotangent, "head", 1)
    from_next = ring_shift(cotangent, "head", -1)
    far = ring_shift(cotangent, "head", 2)
    nt = (((1,), (1,)), ((), ()))
    acc = None
    for piece, group in ((cotangent, me), (from_prev, me - 1), (from_next, me + 1), (far, me + 2)):
        w_cols = head_slice(out_weight, group % groups, width)
        part = lax.dot_general(piece, w_cols, nt, preferred_element_type=jnp.float32)
        acc = part if acc is None else acc + part
    return acc.astype(jnp.bfloat16)


def project_out(attn, out_weight):
    groups = lax.axis_size("head")
    me = lax.axis_index("head")
    _, width = attn.shape

    def part(group):
        w_cols = head_slice(out_weight, group % groups, width)
        return jnp.dot(attn, w_cols, preferred_element_type=jnp.float32).astype(jnp.bfloat16)

    far = part(me + 2)
    near_up = part(me + 1)
    near_down = part(me - 1)
    got_far = ring_shift(far, "head", 2)
    from_prev = ring_shift(near_up, "head", 1)
    from_next = ring_shift(near_down, "head", -1)
    total = (
        jnp.dot(attn, head_slice(out_weight, me, width), preferred_element_type=jnp.float32)
        + from_prev.astype(jnp.float32)
        + from_next.astype(jnp.float32)
        + got_far.astype(jnp.float32)
    )
    return total.astype(jnp.bfloat16)


def partner_swap(block, axis):
    size = lax.axis_size(axis)
    return lax.ppermute(block, axis, [(i, i ^ 1) for i in range(size)])


def even_to_odd(block, axis):
    size = lax.axis_size(axis)
    return lax.ppermute(block, axis, [(i, i + 1) for i in range(0, size - 1, 2)])


def odd_to_even(block, axis):
    size = lax.axis_size(axis)
    return lax.ppermute(block, axis, [(i, i - 1) for i in range(1, size, 2)])


def attn_kernel(sel_ref, q_ref, k0_ref, v0_ref, *refs):
    n_cand = 5
    cand_k = refs[0:2 * n_cand:2]
    cand_v = refs[1:2 * n_cand:2]
    g_ref, srow_ref, scol_ref, attn_ref, dq_ref, self_ref, near_ref, far_ref = refs[2 * n_cand:]
    scale = HEAD_DIM ** (-0.5)

    def pick(cands, slot):
        idx = sel_ref[slot]
        out = cands[0][...]
        for c in range(1, n_cand):
            out = jnp.where(idx == c, cands[c][...], out)
        return out

    ks = [k0_ref[...], pick(cand_k, 0), pick(cand_k, 1)]
    vs = [v0_ref[...], pick(cand_v, 0), pick(cand_v, 1)]
    q = q_ref[...]
    g = g_ref[...]
    nt = (((1,), (1,)), ((), ()))
    tn = (((0,), (0,)), ((), ()))
    scores = [lax.dot_general(q, k, nt, preferred_element_type=jnp.float32) * scale for k in ks]
    visible = srow_ref[...] == scol_ref[...]
    scores[0] = jnp.where(visible, scores[0], NEG_BIG)
    top = jnp.max(scores[0], axis=1, keepdims=True)
    for s in scores[1:]:
        top = jnp.maximum(top, jnp.max(s, axis=1, keepdims=True))
    weights = [jnp.exp(s - top) for s in scores]
    weights[0] = jnp.where(visible, weights[0], 0.0)
    total = weights[0].sum(axis=1, keepdims=True)
    for w in weights[1:]:
        total = total + w.sum(axis=1, keepdims=True)
    inv = 1.0 / total
    probs = [w * inv for w in weights]
    low = [p.astype(jnp.bfloat16) for p in probs]
    acc = jnp.dot(low[0], vs[0], preferred_element_type=jnp.float32)
    for j in (1, 2):
        acc = acc + jnp.dot(low[j], vs[j], preferred_element_type=jnp.float32)
    attn = acc.astype(jnp.bfloat16)
    attn_ref[...] = attn
    gf = g.astype(jnp.float32)
    delta = jnp.sum(attn.astype(jnp.float32) * gf, axis=1, keepdims=True)
    dq = None
    routed = []
    for j in range(3):
        dp = lax.dot_general(g, vs[j], nt, preferred_element_type=jnp.float32)
        ds = (probs[j] * (dp - delta) * scale).astype(jnp.bfloat16)
        part = jnp.dot(ds, ks[j], preferred_element_type=jnp.float32)
        dq = part if dq is None else dq + part
        dk = lax.dot_general(ds, q, tn, preferred_element_type=jnp.float32)
        dv = lax.dot_general(low[j], g, tn, preferred_element_type=jnp.float32)
        if j == 0:
            self_ref[0] = dk
            self_ref[1] = dv
        else:
            routed.append((sel_ref[2 + j], dk.astype(jnp.bfloat16), dv.astype(jnp.bfloat16)))
    (off1, dk1, dv1), (off2, dk2, dv2) = routed
    zero = jnp.zeros_like(dk1)
    for ref, slot, value in ((far_ref, 0, -2), (near_ref, 0, -1), (near_ref, 1, 1), (far_ref, 1, 2)):
        ref[slot, 0] = jnp.where(off1 == value, dk1, jnp.where(off2 == value, dk2, zero))
        ref[slot, 1] = jnp.where(off1 == value, dv1, jnp.where(off2 == value, dv2, zero))
    dq_ref[...] = dq.astype(jnp.bfloat16)


def attention(sel, queries, keys, values, cands, grad_attn, shot_ids):
    rows, columns = queries.shape
    heads = columns // HEAD_DIM
    d = HEAD_DIM
    spec_q = pl.BlockSpec((rows, d), lambda h, s: (0, h))
    spec_ck = pl.BlockSpec((None, rows, d), lambda h, s: (0, 0, h))
    spec_cv = pl.BlockSpec((None, rows, d), lambda h, s: (1, 0, h))
    spec_self = pl.BlockSpec((2, rows, d), lambda h, s: (0, 0, h))
    spec_terms = pl.BlockSpec((2, 2, rows, d), lambda h, s: (0, 0, 0, h))
    cand_specs = []
    cand_args = []
    for c in cands:
        cand_specs += [spec_ck, spec_cv]
        cand_args += [c, c]
    grid_spec = pltpu.PrefetchScalarGridSpec(
        num_scalar_prefetch=1,
        grid=(heads,),
        in_specs=[spec_q, spec_q, spec_q] + cand_specs + [spec_q,
                  pl.BlockSpec((rows, 1), lambda h, s: (0, 0)),
                  pl.BlockSpec((1, rows), lambda h, s: (0, 0))],
        out_specs=[spec_q, spec_q, spec_self, spec_terms, spec_terms],
    )
    out_shape = [
        jax.ShapeDtypeStruct((rows, columns), jnp.bfloat16),
        jax.ShapeDtypeStruct((rows, columns), jnp.bfloat16),
        jax.ShapeDtypeStruct((2, rows, columns), jnp.float32),
        jax.ShapeDtypeStruct((2, 2, rows, columns), jnp.bfloat16),
        jax.ShapeDtypeStruct((2, 2, rows, columns), jnp.bfloat16),
    ]
    kwargs = {}
    if INTERPRET is not None:
        kwargs["interpret"] = INTERPRET
    return pl.pallas_call(
        attn_kernel,
        grid_spec=grid_spec,
        out_shape=out_shape,
        compiler_params=pltpu.CompilerParams(vmem_limit_bytes=48 * 1024 * 1024),
        **kwargs,
    )(sel, queries, keys, values, *cand_args, grad_attn, shot_ids.reshape(rows, 1), shot_ids.reshape(1, rows))


def on_device(queries, keys, values, out_weight, cotangent, routes, shot_ids):
    seq_index = lax.axis_index("seq")
    parity = seq_index % 2
    grad_attn = fold_cotangent(cotangent, out_weight)
    own_kv = jnp.stack([keys, values])
    from_left2 = shifted(own_kv, "seq", 2)
    from_right2 = shifted(own_kv, "seq", -2)
    partner_own = partner_swap(own_kv, "seq")
    relay_to_odd = even_to_odd(from_right2, "seq")
    relay_to_even = odd_to_even(from_left2, "seq")
    partner_off = 1 - 2 * parity
    offs = (routes[seq_index] - seq_index).astype(jnp.int32)
    relay_idx = jnp.where(parity == 1, 2, 3)
    pick = jnp.where(offs == -2, 0, jnp.where(offs == 2, 4, jnp.where(offs == partner_off, 1, relay_idx)))
    sel = jnp.concatenate([pick.astype(jnp.int32), jnp.zeros((1,), jnp.int32), offs])
    cands = (from_left2, partner_own, relay_to_odd, relay_to_even, from_right2)
    attn, grad_q, self_term, near, far = attention(sel, queries, keys, values, cands, grad_attn, shot_ids)
    attn_out = project_out(attn, out_weight)
    got = partner_swap(near, "seq").astype(jnp.float32)
    odd = parity == 1
    up_plus = (far[1].astype(jnp.float32) + jnp.where(odd, 0.0, got[1])).astype(jnp.bfloat16)
    up_minus = (far[0].astype(jnp.float32) + jnp.where(odd, got[0], 0.0)).astype(jnp.bfloat16)
    got_from_left = shifted(up_plus, "seq", 2)
    got_from_right = shifted(up_minus, "seq", -2)

    def summed(part):
        total = (
            self_term[part]
            + jnp.where(odd, got[1, part], got[0, part])
            + got_from_left[part].astype(jnp.float32)
            + got_from_right[part].astype(jnp.float32)
        )
        return total.astype(jnp.bfloat16)

    return (attn_out, grad_q, summed(0), summed(1))


def solution(mesh):
    in_specs = (
        P("seq", "head"),
        P("seq", "head"),
        P("seq", "head"),
        P("head", None),
        P("seq", "head"),
        P(),
        P("seq"),
    )
    out_specs = (P("seq", "head"), P("seq", "head"), P("seq", "head"), P("seq", "head"))

    return jax.shard_map(on_device, mesh=mesh, in_specs=in_specs, out_specs=out_specs, check_vma=False)
```
